32 devices in a mesh: dp: 4 (over z), ctx: 8 (over y, x, core).
Axes of the slice: x: 2, y: 2, z: 4, core: 2. Of those that a mesh axis runs over, the one named last changes fastest.
Arguments:
- tokens: bfloat16 [4, 1024, 6144], P('dp', 'ctx'), may hold values from -0.1875 to 0.1875
- cotangent: bfloat16 [4, 1024, 6144], P('dp', 'ctx'), may hold values from -6 to 6
- w_router: float32 [6144], replicated, may hold values from -2 to 2
- w_query: bfloat16 [6144, 4096], P(None, 'ctx'), may hold values from -0.078125 to 0.078125
- w_key: bfloat16 [6144, 4096], P(None, 'ctx'), may hold values from -0.078125 to 0.078125
- w_value: bfloat16 [6144, 4096], P(None, 'ctx'), may hold values from -0.078125 to 0.078125
- w_out: bfloat16 [4096, 6144], P('ctx'), may hold values from -0.09375 to 0.09375
- chosen: int32 [4, 160], P('dp', 'ctx'), may hold values from -1 to 1023, as said below
- counts: int32 [4, 8], P('dp', 'ctx'), may hold values from 12 to 20, as said below
Outputs:
- layer_out: bfloat16 [4, 1024, 6144], P('dp', 'ctx')
- grad_query: bfloat16 [6144, 4096], P('dp', 'ctx')
- grad_key: bfloat16 [6144, 4096], P('dp', 'ctx')
- grad_value: bfloat16 [6144, 4096], P('dp', 'ctx')
- grad_out: bfloat16 [4096, 6144], P('ctx', 'dp')
- grad_router: float32 [6144], replicated
The draws below stay inside these ranges and needn't reach their ends.
Inputs may be any that keep to these rules, and one draw needn't show every extreme that they name: `chosen`: for every sequence b and device block c, the first counts[b, c] of the block's slots c * 20 to (c + 1) * 20 - 1 hold increasing positions of that device's tokens, c * 128 to (c + 1) * 128 - 1; the other slots hold -1. In every sequence the counts add up to 128, and some device's block has exactly 20 used slots.
All inputs are finite; a program needn't handle non-finite values.
Results may differ from the reference program's by a relative error of at most 0.018.
Values may be sent and summed in bfloat16 or wider, within the bound.
No kernel may reach another device: no remote copies, remote signals or barrier semaphores. Data moves between devices by JAX's collectives and lax.ppermute only.
A program may use at most 128 MiB of HBM per device.

```python
import math
import jax
import jax.numpy as jnp
from jax import lax

D = 6144
HEADS = 32
HDIM = 128
T_DEV = 128
SEL_DEV = 16
CAP = 20
HPD = 4
SEQ_LEN = 1024
SEQS = 4
N_DP = 4
N_CTX = 8


def select_plan(key):
    pairs = N_CTX // 2
    extra = CAP - SEL_DEV
    shifts = jax.random.randint(jax.random.fold_in(key, 11), (N_DP, pairs), 0, extra + 1)
    forced = jax.random.randint(jax.random.fold_in(key, 12), (N_DP, 1), 0, pairs)
    shifts = jnp.where(jnp.arange(pairs, dtype=jnp.int32)[None, :] == forced, extra, shifts)
    flips = jax.random.randint(jax.random.fold_in(key, 13), (N_DP, pairs), 0, 2)
    first = SEL_DEV + shifts * (1 - 2 * flips)
    second = 2 * SEL_DEV - first
    counts = jnp.stack([first, second], axis=-1).reshape(N_DP, N_CTX).astype(jnp.int32)
    places = jnp.arange(T_DEV, dtype=jnp.int32)
    order_keys = jax.random.randint(jax.random.fold_in(key, 14), (N_DP, N_CTX, T_DEV), 0, 65536) * T_DEV + places[None, None, :]
    ranks = jnp.argsort(jnp.argsort(order_keys, axis=-1), axis=-1)
    picked = ranks < counts[:, :, None]
    sort_keys = jnp.where(picked, places[None, None, :], T_DEV + places[None, None, :])
    leading = jnp.argsort(sort_keys, axis=-1)[:, :, :CAP].astype(jnp.int32)
    slot_ids = jnp.arange(CAP, dtype=jnp.int32)
    starts = jnp.arange(N_CTX, dtype=jnp.int32)[None, :, None] * T_DEV
    positions = jnp.where(slot_ids[None, None, :] < counts[:, :, None], leading + starts, -1)
    return (positions.reshape(N_DP, N_CTX * CAP).astype(jnp.int32), counts)


def draw_chosen(key, part):
    return select_plan(key)[0]


def draw_counts(key, part):
    return select_plan(key)[1]


def shard_levels(key, extent, pieces, least, largest):
    def one(position, parts):
        draws = jax.random.uniform(jax.random.fold_in(jax.random.fold_in(key, 6), position), (parts,), jnp.float32, least / len(pieces), largest / len(pieces))
        return jnp.repeat(jnp.exp(draws), extent[position] // parts).reshape((-1,) + (1,) * (len(extent) - position - 1))

    level = one(*pieces[0])
    for cut in pieces[1:]:
        level = level * one(*cut)
    return level


def centred(key, shape, scale, bound, pieces=(), kind=jnp.bfloat16):
    drawn = jax.random.normal(key, shape, jnp.float32) * scale
    if len(pieces) > 0:
        drawn = shard_levels(key, shape, pieces, -0.22, 0.18) * drawn
    return jnp.clip(drawn, min=-bound, max=bound).astype(kind)


def setup_inputs(seed: int = 0) -> dict:
    streams_of = jax.random.split(jax.random.key(seed), 10)
    tokens = centred(streams_of[0], (SEQS, SEQ_LEN, D), 0.03, 0.1875, ((0, 4), (1, 8)))
    cotangent = centred(streams_of[1], (SEQS, SEQ_LEN, D), 1.0, 6.0, ((0, 4), (1, 8)))
    w_router = centred(streams_of[2], (D,), (30.0 * D ** -0.5), 2.0, (), jnp.float32)
    w_query = centred(streams_of[3], (D, HEADS * HDIM), D ** -0.5, 0.078125, ((1, 8),))
    w_key = centred(streams_of[4], (D, HEADS * HDIM), D ** -0.5, 0.078125, ((1, 8),))
    w_value = centred(streams_of[5], (D, HEADS * HDIM), D ** -0.5, 0.078125, ((1, 8),))
    w_out = centred(streams_of[6], (HEADS * HDIM, D), (HEADS * HDIM) ** -0.5, 0.09375, ((0, 8),))
    chosen = draw_chosen(jax.random.fold_in(streams_of[9], 71), 0)
    counts = draw_counts(jax.random.fold_in(streams_of[9], 71), 0)
    return dict(tokens=tokens, cotangent=cotangent, w_router=w_router, w_query=w_query, w_key=w_key, w_value=w_value, w_out=w_out, chosen=chosen, counts=counts)


HIGHEST_PRECISION = lax.Precision.HIGHEST

def head_norm(values, width):
    shaped = values.reshape(values.shape[0], -1, width)
    inverse = lax.rsqrt(lax.optimization_barrier(jnp.mean(shaped * shaped, axis=-1, keepdims=True)) + 1e-06)
    return (shaped * inverse, inverse)

def norm_back(grad_hat, normal, inverse):
    return inverse * (grad_hat - normal * lax.optimization_barrier(jnp.mean(grad_hat * normal, axis=-1, keepdims=True)))

def rounded_sum(total, part):
    return total + lax.optimization_barrier(part.astype(jnp.bfloat16)).astype(jnp.float32)

def reference(tokens, cotangent, w_router, w_query, w_key, w_value, w_out, chosen, counts):
    slots = N_CTX * CAP
    inner = HEADS * HDIM
    block = HPD * HDIM
    scale = 1.0 / math.sqrt(HDIM)
    slot_ids = jnp.arange(slots, dtype=jnp.int32)
    owner = slot_ids // CAP
    within = slot_ids % CAP
    causal = slot_ids[None, :] <= slot_ids[:, None]
    itself = slot_ids[None, :] == slot_ids[:, None]
    outputs = []
    query_total = jnp.zeros((D, inner), jnp.float32)
    key_total = jnp.zeros((D, inner), jnp.float32)
    value_total = jnp.zeros((D, inner), jnp.float32)
    out_total = jnp.zeros((inner, D), jnp.float32)
    router_total = jnp.zeros((D,), jnp.float32)
    for batch in range(N_DP):
        positions = chosen[batch]
        valid = (within < counts[batch][owner]) & (positions >= owner * T_DEV) & (positions < (owner + 1) * T_DEV)
        indices = jnp.where(valid, positions, 0).astype(jnp.int32)
        rows = jnp.where(valid[:, None], tokens[batch][indices].astype(jnp.float32), 0.0)
        rows_back = jnp.where(valid[:, None], cotangent[batch][indices].astype(jnp.float32), 0.0)
        logits = jnp.dot(rows, w_router, precision=HIGHEST_PRECISION)
        weights = jax.nn.sigmoid(logits)
        normed = (rows * lax.rsqrt(lax.optimization_barrier(jnp.mean(rows * rows, axis=-1, keepdims=True)) + 1e-05)).astype(jnp.bfloat16)
        delta = (weights[:, None] * rows_back).astype(jnp.bfloat16)
        query_raw = jnp.dot(normed, w_query, preferred_element_type=jnp.float32)
        key_raw = jnp.dot(normed, w_key, preferred_element_type=jnp.float32)
        value_raw = jnp.dot(normed, w_value, preferred_element_type=jnp.float32)
        query_hat, query_scale = head_norm(query_raw, HDIM)
        key_hat, key_scale = head_norm(key_raw, HDIM)
        query_b = query_hat.astype(jnp.bfloat16)
        key_b = key_hat.astype(jnp.bfloat16)
        value_b = value_raw.reshape(slots, HEADS, HDIM).astype(jnp.bfloat16)
        allowed = causal & (valid[None, :] | itself)
        scores = jnp.einsum('ihd,jhd->hij', query_b.astype(jnp.float32), key_b.astype(jnp.float32)) * scale
        exponent = jnp.where(allowed[None], jnp.exp(scores), 0.0)
        attend = exponent / lax.optimization_barrier(jnp.sum(exponent, axis=-1, keepdims=True))
        attend_b = attend.astype(jnp.bfloat16)
        mixed = jnp.einsum('hij,jhd->ihd', attend_b.astype(jnp.float32), value_b.astype(jnp.float32))
        mixed = mixed.astype(jnp.bfloat16).reshape(slots, inner)
        update = jnp.zeros((slots, D), jnp.float32)
        for group in range(N_CTX):
            part = jnp.dot(mixed[:, group * block:(group + 1) * block], w_out[group * block:(group + 1) * block], preferred_element_type=jnp.float32)
            update = rounded_sum(update, part)
        scaled = jnp.where(valid[:, None], weights[:, None] * update, 0.0)
        merged = tokens[batch].astype(jnp.float32).at[indices].add(scaled)
        outputs.append(merged.astype(jnp.bfloat16))
        gate_back = lax.optimization_barrier(jnp.sum(rows_back * update, axis=-1)) * weights * (1.0 - weights)
        router_total = router_total + jnp.dot(gate_back, rows, precision=HIGHEST_PRECISION)
        out_part = jnp.dot(mixed.T, delta, preferred_element_type=jnp.float32)
        mixed_back = jnp.dot(delta, w_out.T, preferred_element_type=jnp.float32).astype(jnp.bfloat16).reshape(slots, HEADS, HDIM)
        attend_back = jnp.einsum('ihd,jhd->hij', mixed_back.astype(jnp.float32), value_b.astype(jnp.float32))
        inner_sum = lax.optimization_barrier(jnp.sum(attend * attend_back, axis=-1, keepdims=True))
        scores_back = (attend * (attend_back - inner_sum) * scale).astype(jnp.bfloat16)
        value_back = jnp.einsum('hij,ihd->jhd', attend_b.astype(jnp.float32), mixed_back.astype(jnp.float32))
        value_back = value_back.astype(jnp.bfloat16).reshape(slots, inner)
        qhat_back = jnp.einsum('hij,jhd->ihd', scores_back.astype(jnp.float32), key_b.astype(jnp.float32))
        khat_back = jnp.einsum('hij,ihd->jhd', scores_back.astype(jnp.float32), query_b.astype(jnp.float32))
        query_back = norm_back(qhat_back, query_hat, query_scale).astype(jnp.bfloat16).reshape(slots, inner)
        key_back = norm_back(khat_back, key_hat, key_scale).astype(jnp.bfloat16).reshape(slots, inner)
        query_total = rounded_sum(query_total, jnp.dot(normed.T, query_back, preferred_element_type=jnp.float32))
        key_total = rounded_sum(key_total, jnp.dot(normed.T, key_back, preferred_element_type=jnp.float32))
        value_total = rounded_sum(value_total, jnp.dot(normed.T, value_back, preferred_element_type=jnp.float32))
        out_total = rounded_sum(out_total, out_part)
    layer_out = jnp.stack(outputs, axis=0)
    return (layer_out, query_total.astype(jnp.bfloat16), key_total.astype(jnp.bfloat16), value_total.astype(jnp.bfloat16), out_total.astype(jnp.bfloat16), router_total)
```

```python
import math

import jax
import jax.numpy as jnp
from jax import lax
from jax.sharding import PartitionSpec as P

HDIM = 128


HIGHEST_PRECISION = lax.Precision.HIGHEST


def head_norm(values, width):
    shaped = values.reshape(values.shape[0], -1, width)
    inverse = lax.rsqrt(jnp.mean(shaped * shaped, axis=-1, keepdims=True) + 1e-06)
    return (shaped * inverse, inverse)


def norm_back(grad_hat, normal, inverse):
    return inverse * (grad_hat - normal * jnp.mean(grad_hat * normal, axis=-1, keepdims=True))


def rounded_term(part):
    return lax.optimization_barrier(part.astype(jnp.bfloat16)).astype(jnp.float32)


def to_bf16_grid(values):
    return lax.reduce_precision(values, exponent_bits=8, mantissa_bits=7)


def summed_parts(left, right):
    parts = jnp.einsum("bsm,bsn->bmn", left, right, preferred_element_type=jnp.float32)
    return jnp.sum(to_bf16_grid(parts), axis=0).astype(jnp.bfloat16)


def body(n_dp, n_ctx, tokens, cotangent, w_router, w_query, w_key, w_value, w_out, chosen, counts):
    length = tokens.shape[1]
    width = tokens.shape[2]
    capacity = chosen.shape[1]
    inner = w_query.shape[1]
    heads_here = inner // HDIM
    scale = 1.0 / math.sqrt(HDIM)
    offset = lax.axis_index("ctx") * length
    slot_ids = lax.broadcasted_iota(jnp.int32, (capacity,), 0)
    local = chosen[0] - offset
    present = (slot_ids < counts[0, 0]) & (local >= 0) & (local < length)
    columns = lax.broadcasted_iota(jnp.int32, (capacity, length), 1)
    onehot = ((local[:, None] == columns) & present[:, None]).astype(jnp.bfloat16)
    rows = jnp.dot(onehot, tokens[0], preferred_element_type=jnp.float32)
    rows_back = jnp.dot(onehot, cotangent[0], preferred_element_type=jnp.float32)
    logits = jnp.dot(rows, w_router, precision=HIGHEST_PRECISION)
    weights = jax.nn.sigmoid(logits)
    normed = (rows * lax.rsqrt(jnp.mean(rows * rows, axis=-1, keepdims=True) + 1e-05)).astype(
        jnp.bfloat16
    )
    delta = (weights[:, None] * rows_back).astype(jnp.bfloat16)
    flag_row = jnp.zeros((1, width), jnp.bfloat16).at[0, :capacity].set(
        present.astype(jnp.bfloat16)
    )
    packed = lax.all_gather(
        jnp.concatenate([normed, flag_row], axis=0), "ctx", axis=0, tiled=False
    )
    all_normed = packed[:, :capacity].reshape(n_ctx * capacity, width)
    all_present = packed[:, capacity, :capacity].reshape(n_ctx * capacity)
    all_delta = lax.all_gather(delta, "ctx", axis=0, tiled=True)
    slots = all_normed.shape[0]
    query_raw = jnp.dot(all_normed, w_query, preferred_element_type=jnp.float32)
    key_raw = jnp.dot(all_normed, w_key, preferred_element_type=jnp.float32)
    value_raw = jnp.dot(all_normed, w_value, preferred_element_type=jnp.float32)
    query_hat, query_scale = head_norm(query_raw, HDIM)
    key_hat, key_scale = head_norm(key_raw, HDIM)
    query_b = query_hat.astype(jnp.bfloat16)
    key_b = key_hat.astype(jnp.bfloat16)
    value_b = value_raw.reshape(slots, heads_here, HDIM).astype(jnp.bfloat16)
    current = lax.broadcasted_iota(jnp.int32, (slots, slots), 0)
    earlier = lax.broadcasted_iota(jnp.int32, (slots, slots), 1)
    allowed = (earlier <= current) & ((all_present[None, :] > 0.5) | (earlier == current))
    scores = jnp.einsum("ihd,jhd->hij", query_b, key_b, preferred_element_type=jnp.float32) * scale
    exponent = jnp.where(allowed[None], jnp.exp(scores), 0.0)
    attend = exponent / jnp.sum(exponent, axis=-1, keepdims=True)
    attend_b = attend.astype(jnp.bfloat16)
    mixed = jnp.einsum("hij,jhd->ihd", attend_b, value_b, preferred_element_type=jnp.float32)
    mixed = mixed.astype(jnp.bfloat16).reshape(slots, inner)
    update = lax.psum_scatter(
        rounded_term(jnp.dot(mixed, w_out, preferred_element_type=jnp.float32)).astype(
            jnp.bfloat16
        ),
        "ctx",
        scatter_dimension=0,
        tiled=True,
    ).astype(jnp.float32)
    scaled = weights[:, None] * update
    spread = jnp.dot(onehot.astype(jnp.float32).T, scaled, precision=HIGHEST_PRECISION)
    layer_out = (tokens[0].astype(jnp.float32) + spread).astype(jnp.bfloat16)[None]
    gate_back = jnp.sum(rows_back * update, axis=-1) * weights * (1.0 - weights)
    router_part = jnp.dot(gate_back, rows, precision=HIGHEST_PRECISION)
    grad_router = jnp.sum(lax.all_gather(router_part, ("dp", "ctx"), axis=0), axis=0)
    mixed_back = lax.dot_general(
        all_delta, w_out, (((1,), (1,)), ((), ())), preferred_element_type=jnp.float32
    )
    mixed_back = mixed_back.astype(jnp.bfloat16).reshape(slots, heads_here, HDIM)
    attend_back = jnp.einsum(
        "ihd,jhd->hij", mixed_back, value_b, preferred_element_type=jnp.float32
    )
    inner_sum = jnp.sum(attend * attend_back, axis=-1, keepdims=True)
    scores_back = (attend * (attend_back - inner_sum) * scale).astype(jnp.bfloat16)
    value_back = jnp.einsum(
        "hij,ihd->jhd", attend_b, mixed_back, preferred_element_type=jnp.float32
    )
    value_back = value_back.astype(jnp.bfloat16).reshape(slots, inner)
    qhat_back = jnp.einsum("hij,jhd->ihd", scores_back, key_b, preferred_element_type=jnp.float32)
    khat_back = jnp.einsum("hij,ihd->jhd", scores_back, query_b, preferred_element_type=jnp.float32)
    query_back = (
        norm_back(qhat_back, query_hat, query_scale).astype(jnp.bfloat16).reshape(slots, inner)
    )
    key_back = norm_back(khat_back, key_hat, key_scale).astype(jnp.bfloat16).reshape(slots, inner)
    block = width // n_dp
    factors = lax.all_gather(
        jnp.stack([query_back, key_back, value_back, mixed]), "dp", axis=0, tiled=False
    )
    blocks = lax.all_to_all(
        jnp.stack([all_normed, all_delta]).reshape(2, slots, n_dp, block).transpose(2, 0, 1, 3),
        "dp",
        0,
        0,
        tiled=True,
    )
    normed_blocks = blocks[:, 0]
    delta_blocks = blocks[:, 1]
    grad_query = summed_parts(normed_blocks, factors[:, 0])
    grad_key = summed_parts(normed_blocks, factors[:, 1])
    grad_value = summed_parts(normed_blocks, factors[:, 2])
    grad_out = summed_parts(factors[:, 3], delta_blocks)
    return (layer_out, grad_query, grad_key, grad_value, grad_out, grad_router)


def solution(mesh):
    n_dp = mesh.shape["dp"]
    n_ctx = mesh.shape["ctx"]
    in_specs = (
        P("dp", "ctx", None),
        P("dp", "ctx", None),
        P(),
        P(None, "ctx"),
        P(None, "ctx"),
        P(None, "ctx"),
        P("ctx", None),
        P("dp", "ctx"),
        P("dp", "ctx"),
    )
    out_specs = (
        P("dp", "ctx", None),
        P("dp", "ctx"),
        P("dp", "ctx"),
        P("dp", "ctx"),
        P("ctx", "dp"),
        P(),
    )

    def run(*args):
        return body(n_dp, n_ctx, *args)

    return jax.shard_map(run, mesh=mesh, in_specs=in_specs, out_specs=out_specs, check_vma=False)
```

```python
import math

import jax
import jax.numpy as jnp
from jax import lax
from jax.sharding import PartitionSpec as P

HDIM = 128


HIGHEST_PRECISION = lax.Precision.HIGHEST


def head_norm(values, width):
    shaped = values.reshape(values.shape[0], -1, width)
    inverse = lax.rsqrt(jnp.mean(shaped * shaped, axis=-1, keepdims=True) + 1e-06)
    return (shaped * inverse, inverse)


def norm_back(grad_hat, normal, inverse):
    return inverse * (grad_hat - normal * jnp.mean(grad_hat * normal, axis=-1, keepdims=True))


def rounded_term(part):
    return lax.optimization_barrier(part.astype(jnp.bfloat16)).astype(jnp.float32)


def body(n_dp, n_ctx, tokens, cotangent, w_router, w_query, w_key, w_value, w_out, chosen, counts):
    length = tokens.shape[1]
    width = tokens.shape[2]
    capacity = chosen.shape[1]
    inner = w_query.shape[1]
    heads_here = inner // HDIM
    scale = 1.0 / math.sqrt(HDIM)
    offset = lax.axis_index("ctx") * length
    slot_ids = lax.broadcasted_iota(jnp.int32, (capacity,), 0)
    local = chosen[0] - offset
    present = (slot_ids < counts[0, 0]) & (local >= 0) & (local < length)
    columns = lax.broadcasted_iota(jnp.int32, (capacity, length), 1)
    onehot = ((local[:, None] == columns) & present[:, None]).astype(jnp.bfloat16)
    rows = jnp.dot(onehot, tokens[0], preferred_element_type=jnp.float32)
    rows_back = jnp.dot(onehot, cotangent[0], preferred_element_type=jnp.float32)
    logits = jnp.dot(rows, w_router, precision=HIGHEST_PRECISION)
    weights = jax.nn.sigmoid(logits)
    normed = (rows * lax.rsqrt(jnp.mean(rows * rows, axis=-1, keepdims=True) + 1e-05)).astype(
        jnp.bfloat16
    )
    delta = (weights[:, None] * rows_back).astype(jnp.bfloat16)
    flag_cols = jnp.zeros((capacity, HDIM), jnp.bfloat16).at[:, 0].set(
        present.astype(jnp.bfloat16)
    )
    packed = lax.all_gather(
        jnp.concatenate([normed, delta, flag_cols], axis=1), "ctx", axis=0, tiled=True
    )
    all_normed = packed[:, :width]
    all_delta = packed[:, width : 2 * width]
    all_present = packed[:, 2 * width]
    slots = all_normed.shape[0]
    query_raw = jnp.dot(all_normed, w_query, preferred_element_type=jnp.float32)
    key_raw = jnp.dot(all_normed, w_key, preferred_element_type=jnp.float32)
    value_raw = jnp.dot(all_normed, w_value, preferred_element_type=jnp.float32)
    query_hat, query_scale = head_norm(query_raw, HDIM)
    key_hat, key_scale = head_norm(key_raw, HDIM)
    query_b = query_hat.astype(jnp.bfloat16)
    key_b = key_hat.astype(jnp.bfloat16)
    value_b = value_raw.reshape(slots, heads_here, HDIM).astype(jnp.bfloat16)
    current = lax.broadcasted_iota(jnp.int32, (slots, slots), 0)
    earlier = lax.broadcasted_iota(jnp.int32, (slots, slots), 1)
    allowed = (earlier <= current) & ((all_present[None, :] > 0.5) | (earlier == current))
    scores = jnp.einsum("ihd,jhd->hij", query_b, key_b, preferred_element_type=jnp.float32) * scale
    exponent = jnp.where(allowed[None], jnp.exp(scores), 0.0)
    attend = exponent / jnp.sum(exponent, axis=-1, keepdims=True)
    attend_b = attend.astype(jnp.bfloat16)
    mixed = jnp.einsum("hij,jhd->ihd", attend_b, value_b, preferred_element_type=jnp.float32)
    mixed = mixed.astype(jnp.bfloat16).reshape(slots, inner)
    contributions = jnp.dot(mixed, w_out, preferred_element_type=jnp.float32).astype(jnp.bfloat16)
    received = lax.all_to_all(
        contributions.reshape(n_ctx, capacity, width), "ctx", 0, 0, tiled=True
    )
    update = jnp.sum(received.astype(jnp.float32), axis=0)
    scaled = weights[:, None] * update
    spread = jnp.dot(onehot.astype(jnp.float32).T, scaled, precision=HIGHEST_PRECISION)
    layer_out = (tokens[0].astype(jnp.float32) + spread).astype(jnp.bfloat16)[None]
    gate_back = jnp.sum(rows_back * update, axis=-1) * weights * (1.0 - weights)
    router_part = jnp.dot(gate_back, rows, precision=HIGHEST_PRECISION)
    router_split = jnp.stack(
        [router_part.astype(jnp.bfloat16), (router_part - router_part.astype(jnp.bfloat16).astype(jnp.float32)).astype(jnp.bfloat16)]
    )
    router_group = jnp.sum(
        lax.all_gather(router_split, "ctx", axis=0, tiled=False).astype(jnp.float32), axis=(0, 1)
    )
    router_high = router_group.astype(jnp.bfloat16)
    router_low = (router_group - router_high.astype(jnp.float32)).astype(jnp.bfloat16)
    mixed_back = lax.dot_general(
        all_delta, w_out, (((1,), (1,)), ((), ())), preferred_element_type=jnp.float32
    )
    mixed_back = mixed_back.astype(jnp.bfloat16).reshape(slots, heads_here, HDIM)
    attend_back = jnp.einsum(
        "ihd,jhd->hij", mixed_back, value_b, preferred_element_type=jnp.float32
    )
    inner_sum = jnp.sum(attend * attend_back, axis=-1, keepdims=True)
    scores_back = (attend * (attend_back - inner_sum) * scale).astype(jnp.bfloat16)
    value_back = jnp.einsum(
        "hij,ihd->jhd", attend_b, mixed_back, preferred_element_type=jnp.float32
    )
    value_back = value_back.astype(jnp.bfloat16).reshape(slots, inner)
    qhat_back = jnp.einsum("hij,jhd->ihd", scores_back, key_b, preferred_element_type=jnp.float32)
    khat_back = jnp.einsum("hij,ihd->jhd", scores_back, query_b, preferred_element_type=jnp.float32)
    query_back = (
        norm_back(qhat_back, query_hat, query_scale).astype(jnp.bfloat16).reshape(slots, inner)
    )
    key_back = norm_back(khat_back, key_hat, key_scale).astype(jnp.bfloat16).reshape(slots, inner)
    router_rows = width // inner
    local_factors = jnp.concatenate(
        [
            query_back,
            key_back,
            value_back,
            mixed,
            router_high.reshape(router_rows, inner),
            router_low.reshape(router_rows, inner),
        ],
        axis=0,
    )
    factors = lax.all_to_all(
        jnp.broadcast_to(local_factors[None], (n_dp,) + local_factors.shape), "dp", 0, 0, tiled=True
    )
    normed_blocks = lax.all_to_all(all_normed, "dp", 1, 0, tiled=True)
    delta_blocks = lax.all_to_all(all_delta, "dp", 1, 0, tiled=True)

    def gathered(index):
        return factors[:, index * slots : (index + 1) * slots].reshape(n_dp * slots, inner)

    def contract(left, right):
        return lax.dot_general(
            left, right, (((0,), (0,)), ((), ())), preferred_element_type=jnp.float32
        ).astype(jnp.bfloat16)

    grad_query = contract(normed_blocks, gathered(0))
    grad_key = contract(normed_blocks, gathered(1))
    grad_value = contract(normed_blocks, gathered(2))
    grad_out = contract(gathered(3), delta_blocks)
    router_pieces = factors[:, 4 * slots :].astype(jnp.float32).reshape(n_dp, 2, width)
    grad_router = jnp.sum(router_pieces[:, 0] + router_pieces[:, 1], axis=0)
    return (layer_out, grad_query, grad_key, grad_value, grad_out, grad_router)


def solution(mesh):
    n_dp = mesh.shape["dp"]
    n_ctx = mesh.shape["ctx"]
    in_specs = (
        P("dp", "ctx", None),
        P("dp", "ctx", None),
        P(),
        P(None, "ctx"),
        P(None, "ctx"),
        P(None, "ctx"),
        P("ctx", None),
        P("dp", "ctx"),
        P("dp", "ctx"),
    )
    out_specs = (
        P("dp", "ctx", None),
        P("dp", "ctx"),
        P("dp", "ctx"),
        P("dp", "ctx"),
        P("ctx", "dp"),
        P(),
    )

    def run(*args):
        return body(n_dp, n_ctx, *args)

    return jax.shard_map(run, mesh=mesh, in_specs=in_specs, out_specs=out_specs, check_vma=False)
```

```python
import math

import jax
import jax.numpy as jnp
from jax import lax
from jax.sharding import PartitionSpec as P

HDIM = 128


HIGHEST_PRECISION = lax.Precision.HIGHEST


def head_norm(values, width):
    shaped = values.reshape(values.shape[0], -1, width)
    inverse = lax.rsqrt(jnp.mean(shaped * shaped, axis=-1, keepdims=True) + 1e-06)
    return (shaped * inverse, inverse)


def norm_back(grad_hat, normal, inverse):
    return inverse * (grad_hat - normal * jnp.mean(grad_hat * normal, axis=-1, keepdims=True))


def rounded_term(part):
    return lax.optimization_barrier(part.astype(jnp.bfloat16)).astype(jnp.float32)


def body(n_dp, n_ctx, tokens, cotangent, w_router, w_query, w_key, w_value, w_out, chosen, counts):
    length = tokens.shape[1]
    width = tokens.shape[2]
    capacity = chosen.shape[1]
    inner = w_query.shape[1]
    heads_here = inner // HDIM
    scale = 1.0 / math.sqrt(HDIM)
    offset = lax.axis_index("ctx") * length
    slot_ids = lax.broadcasted_iota(jnp.int32, (capacity,), 0)
    local = chosen[0] - offset
    present = (slot_ids < counts[0, 0]) & (local >= 0) & (local < length)
    columns = lax.broadcasted_iota(jnp.int32, (capacity, length), 1)
    onehot = ((local[:, None] == columns) & present[:, None]).astype(jnp.bfloat16)
    rows = jnp.dot(onehot, tokens[0], preferred_element_type=jnp.float32)
    rows_back = jnp.dot(onehot, cotangent[0], preferred_element_type=jnp.float32)
    logits = jnp.dot(rows, w_router, precision=HIGHEST_PRECISION)
    weights = jax.nn.sigmoid(logits)
    normed = (rows * lax.rsqrt(jnp.mean(rows * rows, axis=-1, keepdims=True) + 1e-05)).astype(
        jnp.bfloat16
    )
    delta = (weights[:, None] * rows_back).astype(jnp.bfloat16)
    flag_cols = jnp.zeros((capacity, HDIM), jnp.bfloat16).at[:, 0].set(
        present.astype(jnp.bfloat16)
    )
    packed = lax.all_gather(
        jnp.concatenate([normed, delta, flag_cols], axis=1), "ctx", axis=0, tiled=True
    )
    all_normed = packed[:, :width]
    all_delta = packed[:, width : 2 * width]
    all_present = packed[:, 2 * width]
    slots = all_normed.shape[0]
    block = width // n_dp
    own_blocks = lax.all_to_all(
        jnp.concatenate([normed, delta], axis=0), "dp", 1, 0, tiled=True
    )
    pieces = lax.all_gather(own_blocks, "ctx", axis=0, tiled=False).reshape(
        n_ctx, n_dp, 2, capacity, block
    )
    normed_blocks = pieces[:, :, 0].transpose(1, 0, 2, 3).reshape(n_dp * slots, block)
    delta_blocks = pieces[:, :, 1].transpose(1, 0, 2, 3).reshape(n_dp * slots, block)
    query_raw = jnp.dot(all_normed, w_query, preferred_element_type=jnp.float32)
    key_raw = jnp.dot(all_normed, w_key, preferred_element_type=jnp.float32)
    value_raw = jnp.dot(all_normed, w_value, preferred_element_type=jnp.float32)
    query_hat, query_scale = head_norm(query_raw, HDIM)
    key_hat, key_scale = head_norm(key_raw, HDIM)
    query_b = query_hat.astype(jnp.bfloat16)
    key_b = key_hat.astype(jnp.bfloat16)
    value_b = value_raw.reshape(slots, heads_here, HDIM).astype(jnp.bfloat16)
    current = lax.broadcasted_iota(jnp.int32, (slots, slots), 0)
    earlier = lax.broadcasted_iota(jnp.int32, (slots, slots), 1)
    allowed = (earlier <= current) & ((all_present[None, :] > 0.5) | (earlier == current))
    scores = jnp.einsum("ihd,jhd->hij", query_b, key_b, preferred_element_type=jnp.float32) * scale
    exponent = jnp.where(allowed[None], jnp.exp(scores), 0.0)
    attend = exponent / jnp.sum(exponent, axis=-1, keepdims=True)
    attend_b = attend.astype(jnp.bfloat16)
    mixed = jnp.einsum("hij,jhd->ihd", attend_b, value_b, preferred_element_type=jnp.float32)
    mixed = mixed.astype(jnp.bfloat16).reshape(slots, inner)
    contributions = jnp.dot(mixed, w_out, preferred_element_type=jnp.float32).astype(jnp.bfloat16)
    received = lax.all_to_all(
        contributions.reshape(n_ctx, capacity, width), "ctx", 0, 0, tiled=True
    )
    update = jnp.sum(received.astype(jnp.float32), axis=0)
    scaled = weights[:, None] * update
    spread = jnp.dot(onehot.astype(jnp.float32).T, scaled, precision=HIGHEST_PRECISION)
    layer_out = (tokens[0].astype(jnp.float32) + spread).astype(jnp.bfloat16)[None]
    gate_back = jnp.sum(rows_back * update, axis=-1) * weights * (1.0 - weights)
    router_part = jnp.dot(gate_back, rows, precision=HIGHEST_PRECISION)
    router_split = jnp.stack(
        [
            router_part.astype(jnp.bfloat16),
            (router_part - router_part.astype(jnp.bfloat16).astype(jnp.float32)).astype(
                jnp.bfloat16
            ),
        ]
    )
    router_group = jnp.sum(
        lax.all_gather(router_split, "ctx", axis=0, tiled=False).astype(jnp.float32), axis=(0, 1)
    )
    router_high = router_group.astype(jnp.bfloat16)
    router_low = (router_group - router_high.astype(jnp.float32)).astype(jnp.bfloat16)
    mixed_back = lax.dot_general(
        all_delta, w_out, (((1,), (1,)), ((), ())), preferred_element_type=jnp.float32
    )
    mixed_back = mixed_back.astype(jnp.bfloat16).reshape(slots, heads_here, HDIM)
    attend_back = jnp.einsum(
        "ihd,jhd->hij", mixed_back, value_b, preferred_element_type=jnp.float32
    )
    inner_sum = jnp.sum(attend * attend_back, axis=-1, keepdims=True)
    scores_back = (attend * (attend_back - inner_sum) * scale).astype(jnp.bfloat16)
    value_back = jnp.einsum(
        "hij,ihd->jhd", attend_b, mixed_back, preferred_element_type=jnp.float32
    )
    value_back = value_back.astype(jnp.bfloat16).reshape(slots, inner)
    qhat_back = jnp.einsum("hij,jhd->ihd", scores_back, key_b, preferred_element_type=jnp.float32)
    khat_back = jnp.einsum("hij,ihd->jhd", scores_back, query_b, preferred_element_type=jnp.float32)
    query_back = (
        norm_back(qhat_back, query_hat, query_scale).astype(jnp.bfloat16).reshape(slots, inner)
    )
    key_back = norm_back(khat_back, key_hat, key_scale).astype(jnp.bfloat16).reshape(slots, inner)
    factors = lax.all_gather(
        jnp.concatenate(
            [
                query_back,
                key_back,
                value_back,
                mixed,
            ],
            axis=0,
        ),
        "dp",
        axis=0,
        tiled=False,
    )

    def gathered(index):
        return factors[:, index * slots : (index + 1) * slots].reshape(n_dp * slots, inner)

    def contract(left, right):
        return lax.dot_general(
            left, right, (((0,), (0,)), ((), ())), preferred_element_type=jnp.float32
        ).astype(jnp.bfloat16)

    grad_query = contract(normed_blocks, gathered(0))
    grad_key = contract(normed_blocks, gathered(1))
    grad_value = contract(normed_blocks, gathered(2))
    grad_out = contract(gathered(3), delta_blocks)
    router_pieces = lax.all_gather(
        jnp.stack([router_high, router_low]), "dp", axis=0, tiled=False
    ).astype(jnp.float32)
    grad_router = jnp.sum(router_pieces[:, 0] + router_pieces[:, 1], axis=0)
    return (layer_out, grad_query, grad_key, grad_value, grad_out, grad_router)


def solution(mesh):
    n_dp = mesh.shape["dp"]
    n_ctx = mesh.shape["ctx"]
    in_specs = (
        P("dp", "ctx", None),
        P("dp", "ctx", None),
        P(),
        P(None, "ctx"),
        P(None, "ctx"),
        P(None, "ctx"),
        P("ctx", None),
        P("dp", "ctx"),
        P("dp", "ctx"),
    )
    out_specs = (
        P("dp", "ctx", None),
        P("dp", "ctx"),
        P("dp", "ctx"),
        P("dp", "ctx"),
        P("ctx", "dp"),
        P(),
    )

    def run(*args):
        return body(n_dp, n_ctx, *args)

    return jax.shard_map(run, mesh=mesh, in_specs=in_specs, out_specs=out_specs, check_vma=False)
```

```python
import math

import jax
import jax.numpy as jnp
from jax import lax
from jax.sharding import PartitionSpec as P

HDIM = 128


HIGHEST_PRECISION = lax.Precision.HIGHEST


def head_norm(values, width):
    shaped = values.reshape(values.shape[0], -1, width)
    inverse = lax.rsqrt(jnp.mean(shaped * shaped, axis=-1, keepdims=True) + 1e-06)
    return (shaped * inverse, inverse)


def norm_back(grad_hat, normal, inverse):
    return inverse * (grad_hat - normal * jnp.mean(grad_hat * normal, axis=-1, keepdims=True))


def rounded_term(part):
    return lax.optimization_barrier(part.astype(jnp.bfloat16)).astype(jnp.float32)


def body(n_dp, n_ctx, tokens, cotangent, w_router, w_query, w_key, w_value, w_out, chosen, counts):
    length = tokens.shape[1]
    width = tokens.shape[2]
    capacity = chosen.shape[1]
    inner = w_query.shape[1]
    heads_here = inner // HDIM
    scale = 1.0 / math.sqrt(HDIM)
    offset = lax.axis_index("ctx") * length
    slot_ids = lax.broadcasted_iota(jnp.int32, (capacity,), 0)
    local = chosen[0] - offset
    present = (slot_ids < counts[0, 0]) & (local >= 0) & (local < length)
    columns = lax.broadcasted_iota(jnp.int32, (capacity, length), 1)
    onehot = ((local[:, None] == columns) & present[:, None]).astype(jnp.bfloat16)
    rows = jnp.dot(onehot, tokens[0], preferred_element_type=jnp.float32)
    rows_back = jnp.dot(onehot, cotangent[0], preferred_element_type=jnp.float32)
    logits = jnp.dot(rows, w_router, precision=HIGHEST_PRECISION)
    weights = jax.nn.sigmoid(logits)
    normed = (rows * lax.rsqrt(jnp.mean(rows * rows, axis=-1, keepdims=True) + 1e-05)).astype(
        jnp.bfloat16
    )
    delta = (weights[:, None] * rows_back).astype(jnp.bfloat16)
    flag_cols = jnp.zeros((capacity, HDIM), jnp.bfloat16).at[:, 0].set(
        present.astype(jnp.bfloat16)
    )
    packed = lax.all_gather(
        jnp.concatenate([normed, delta, flag_cols], axis=1), "ctx", axis=0, tiled=False
    )
    chunk_normed = packed[:, :, :width]
    chunk_delta = packed[:, :, width : 2 * width]
    all_present = packed[:, :, 2 * width].reshape(n_ctx * capacity)
    slots = n_ctx * capacity
    block = width // n_dp
    own_blocks = lax.all_to_all(
        jnp.concatenate([normed, delta], axis=0), "dp", 1, 0, tiled=True
    )
    pieces = lax.all_gather(own_blocks, "ctx", axis=0, tiled=False).reshape(
        n_ctx, n_dp, 2, capacity, block
    )
    normed_blocks = pieces[:, :, 0].transpose(1, 0, 2, 3).reshape(n_dp * slots, block)
    delta_blocks = pieces[:, :, 1].transpose(1, 0, 2, 3).reshape(n_dp * slots, block)
    def project(weight):
        raw = lax.dot_general(
            chunk_normed, weight, (((2,), (0,)), ((), ())), preferred_element_type=jnp.float32
        )
        return raw.reshape(slots, inner)

    query_raw = project(w_query)
    key_raw = project(w_key)
    value_raw = project(w_value)
    query_hat, query_scale = head_norm(query_raw, HDIM)
    key_hat, key_scale = head_norm(key_raw, HDIM)
    query_b = query_hat.astype(jnp.bfloat16)
    key_b = key_hat.astype(jnp.bfloat16)
    value_b = value_raw.reshape(slots, heads_here, HDIM).astype(jnp.bfloat16)
    current = lax.broadcasted_iota(jnp.int32, (slots, slots), 0)
    earlier = lax.broadcasted_iota(jnp.int32, (slots, slots), 1)
    allowed = (earlier <= current) & ((all_present[None, :] > 0.5) | (earlier == current))
    scores = jnp.einsum("ihd,jhd->hij", query_b, key_b, preferred_element_type=jnp.float32) * scale
    exponent = jnp.where(allowed[None], jnp.exp(scores), 0.0)
    attend = exponent / jnp.sum(exponent, axis=-1, keepdims=True)
    attend_b = attend.astype(jnp.bfloat16)
    mixed = jnp.einsum("hij,jhd->ihd", attend_b, value_b, preferred_element_type=jnp.float32)
    mixed = mixed.astype(jnp.bfloat16).reshape(slots, inner)
    contributions = lax.dot_general(
        mixed.reshape(n_ctx, capacity, inner),
        w_out,
        (((2,), (0,)), ((), ())),
        preferred_element_type=jnp.float32,
    ).astype(jnp.bfloat16)
    received = lax.all_to_all(
        contributions, "ctx", 0, 0, tiled=True
    )
    update = jnp.sum(received.astype(jnp.float32), axis=0)
    scaled = weights[:, None] * update
    spread = jnp.dot(onehot.astype(jnp.float32).T, scaled, precision=HIGHEST_PRECISION)
    layer_out = (tokens[0].astype(jnp.float32) + spread).astype(jnp.bfloat16)[None]
    gate_back = jnp.sum(rows_back * update, axis=-1) * weights * (1.0 - weights)
    router_part = jnp.dot(gate_back, rows, precision=HIGHEST_PRECISION)
    router_split = jnp.stack(
        [
            router_part.astype(jnp.bfloat16),
            (router_part - router_part.astype(jnp.bfloat16).astype(jnp.float32)).astype(
                jnp.bfloat16
            ),
        ]
    )
    router_group = jnp.sum(
        lax.all_gather(router_split, "ctx", axis=0, tiled=False).astype(jnp.float32), axis=(0, 1)
    )
    router_high = router_group.astype(jnp.bfloat16)
    router_low = (router_group - router_high.astype(jnp.float32)).astype(jnp.bfloat16)
    mixed_back = lax.dot_general(
        chunk_delta, w_out, (((2,), (1,)), ((), ())), preferred_element_type=jnp.float32
    )
    mixed_back = mixed_back.astype(jnp.bfloat16).reshape(slots, heads_here, HDIM)
    attend_back = jnp.einsum(
        "ihd,jhd->hij", mixed_back, value_b, preferred_element_type=jnp.float32
    )
    inner_sum = jnp.sum(attend * attend_back, axis=-1, keepdims=True)
    scores_back = (attend * (attend_back - inner_sum) * scale).astype(jnp.bfloat16)
    value_back = jnp.einsum(
        "hij,ihd->jhd", attend_b, mixed_back, preferred_element_type=jnp.float32
    )
    value_back = value_back.astype(jnp.bfloat16).reshape(slots, inner)
    qhat_back = jnp.einsum("hij,jhd->ihd", scores_back, key_b, preferred_element_type=jnp.float32)
    khat_back = jnp.einsum("hij,ihd->jhd", scores_back, query_b, preferred_element_type=jnp.float32)
    query_back = (
        norm_back(qhat_back, query_hat, query_scale).astype(jnp.bfloat16).reshape(slots, inner)
    )
    key_back = norm_back(khat_back, key_hat, key_scale).astype(jnp.bfloat16).reshape(slots, inner)
    factors = lax.all_gather(
        jnp.concatenate(
            [
                query_back,
                key_back,
                value_back,
                mixed,
            ],
            axis=0,
        ),
        "dp",
        axis=0,
        tiled=False,
    )

    def gathered(index):
        return factors[:, index * slots : (index + 1) * slots].reshape(n_dp * slots, inner)

    def contract(left, right):
        return lax.dot_general(
            left, right, (((0,), (0,)), ((), ())), preferred_element_type=jnp.float32
        ).astype(jnp.bfloat16)

    grad_query = contract(normed_blocks, gathered(0))
    grad_key = contract(normed_blocks, gathered(1))
    grad_value = contract(normed_blocks, gathered(2))
    grad_out = contract(gathered(3), delta_blocks)
    router_pieces = lax.all_gather(
        jnp.stack([router_high, router_low]), "dp", axis=0, tiled=False
    ).astype(jnp.float32)
    grad_router = jnp.sum(router_pieces[:, 0] + router_pieces[:, 1], axis=0)
    return (layer_out, grad_query, grad_key, grad_value, grad_out, grad_router)


def solution(mesh):
    n_dp = mesh.shape["dp"]
    n_ctx = mesh.shape["ctx"]
    in_specs = (
        P("dp", "ctx", None),
        P("dp", "ctx", None),
        P(),
        P(None, "ctx"),
        P(None, "ctx"),
        P(None, "ctx"),
        P("ctx", None),
        P("dp", "ctx"),
        P("dp", "ctx"),
    )
    out_specs = (
        P("dp", "ctx", None),
        P("dp", "ctx"),
        P("dp", "ctx"),
        P("dp", "ctx"),
        P("ctx", "dp"),
        P(),
    )

    def run(*args):
        return body(n_dp, n_ctx, *args)

    return jax.shard_map(run, mesh=mesh, in_specs=in_specs, out_specs=out_specs, check_vma=False)
```

```python
import math

import jax
import jax.numpy as jnp
from jax import lax
from jax.sharding import PartitionSpec as P

HDIM = 128


HIGHEST_PRECISION = lax.Precision.HIGHEST


def head_norm(values, width):
    shaped = values.reshape(values.shape[0], -1, width)
    inverse = lax.rsqrt(jnp.mean(shaped * shaped, axis=-1, keepdims=True) + 1e-06)
    return (shaped * inverse, inverse)


def norm_back(grad_hat, normal, inverse):
    return inverse * (grad_hat - normal * jnp.mean(grad_hat * normal, axis=-1, keepdims=True))


def rounded_term(part):
    return lax.optimization_barrier(part.astype(jnp.bfloat16)).astype(jnp.float32)


def body(n_dp, n_ctx, tokens, cotangent, w_router, w_query, w_key, w_value, w_out, chosen, counts):
    length = tokens.shape[1]
    width = tokens.shape[2]
    capacity = chosen.shape[1]
    inner = w_query.shape[1]
    heads_here = inner // HDIM
    scale = 1.0 / math.sqrt(HDIM)
    offset = lax.axis_index("ctx") * length
    slot_ids = lax.broadcasted_iota(jnp.int32, (capacity,), 0)
    local = chosen[0] - offset
    present = (slot_ids < counts[0, 0]) & (local >= 0) & (local < length)
    columns = lax.broadcasted_iota(jnp.int32, (capacity, length), 1)
    onehot = ((local[:, None] == columns) & present[:, None]).astype(jnp.bfloat16)
    rows = jnp.dot(onehot, tokens[0], preferred_element_type=jnp.float32)
    rows_back = jnp.dot(onehot, cotangent[0], preferred_element_type=jnp.float32)
    logits = jnp.dot(rows, w_router, precision=HIGHEST_PRECISION)
    weights = jax.nn.sigmoid(logits)
    normed = (rows * lax.rsqrt(jnp.mean(rows * rows, axis=-1, keepdims=True) + 1e-05)).astype(
        jnp.bfloat16
    )
    delta = (weights[:, None] * rows_back).astype(jnp.bfloat16)
    flag_cols = jnp.zeros((capacity, HDIM), jnp.bfloat16).at[:, 0].set(
        present.astype(jnp.bfloat16)
    )
    packed = lax.all_gather(
        jnp.concatenate([normed, delta, flag_cols], axis=1), "ctx", axis=0, tiled=False
    )
    chunk_normed = packed[:, :, :width]
    chunk_delta = packed[:, :, width : 2 * width]
    all_present = packed[:, :, 2 * width].reshape(n_ctx * capacity)
    slots = n_ctx * capacity
    block = width // n_dp
    own_blocks = lax.all_to_all(
        jnp.concatenate([normed, delta], axis=0), "dp", 1, 0, tiled=True
    )
    pieces = lax.all_gather(own_blocks, "ctx", axis=0, tiled=False).reshape(
        n_ctx, n_dp, 2, capacity, block
    )
    normed_blocks = pieces[:, :, 0].transpose(1, 0, 2, 3).reshape(n_dp * slots, block)
    delta_blocks = pieces[:, :, 1].transpose(1, 0, 2, 3).reshape(n_dp * slots, block)
    def project(weight):
        raw = lax.dot_general(
            chunk_normed, weight, (((2,), (0,)), ((), ())), preferred_element_type=jnp.float32
        )
        return raw.reshape(slots, inner)

    query_raw = project(w_query)
    key_raw = project(w_key)
    value_raw = project(w_value)
    query_hat, query_scale = head_norm(query_raw, HDIM)
    key_hat, key_scale = head_norm(key_raw, HDIM)
    query_b = query_hat.astype(jnp.bfloat16)
    key_b = key_hat.astype(jnp.bfloat16)
    value_b = value_raw.reshape(slots, heads_here, HDIM).astype(jnp.bfloat16)
    current = lax.broadcasted_iota(jnp.int32, (slots, slots), 0)
    earlier = lax.broadcasted_iota(jnp.int32, (slots, slots), 1)
    allowed = (earlier <= current) & ((all_present[None, :] > 0.5) | (earlier == current))
    scores = jnp.einsum("ihd,jhd->hij", query_b, key_b, preferred_element_type=jnp.float32) * scale
    exponent = jnp.where(allowed[None], jnp.exp(scores), 0.0)
    attend = exponent / jnp.sum(exponent, axis=-1, keepdims=True)
    attend_b = attend.astype(jnp.bfloat16)
    mixed = jnp.einsum("hij,jhd->ihd", attend_b, value_b, preferred_element_type=jnp.float32)
    mixed = mixed.astype(jnp.bfloat16).reshape(slots, inner)
    mixed_back = lax.dot_general(
        chunk_delta, w_out, (((2,), (1,)), ((), ())), preferred_element_type=jnp.float32
    )
    mixed_back = mixed_back.astype(jnp.bfloat16).reshape(slots, heads_here, HDIM)
    attend_back = jnp.einsum(
        "ihd,jhd->hij", mixed_back, value_b, preferred_element_type=jnp.float32
    )
    inner_sum = jnp.sum(attend * attend_back, axis=-1, keepdims=True)
    scores_back = (attend * (attend_back - inner_sum) * scale).astype(jnp.bfloat16)
    value_back = jnp.einsum(
        "hij,ihd->jhd", attend_b, mixed_back, preferred_element_type=jnp.float32
    )
    value_back = value_back.astype(jnp.bfloat16).reshape(slots, inner)
    qhat_back = jnp.einsum("hij,jhd->ihd", scores_back, key_b, preferred_element_type=jnp.float32)
    khat_back = jnp.einsum("hij,ihd->jhd", scores_back, query_b, preferred_element_type=jnp.float32)
    query_back = (
        norm_back(qhat_back, query_hat, query_scale).astype(jnp.bfloat16).reshape(slots, inner)
    )
    key_back = norm_back(khat_back, key_hat, key_scale).astype(jnp.bfloat16).reshape(slots, inner)
    mixed_late, query_back, key_back, value_back = lax.optimization_barrier(
        (mixed, query_back, key_back, value_back)
    )
    contributions = lax.dot_general(
        mixed_late.reshape(n_ctx, capacity, inner),
        w_out,
        (((2,), (0,)), ((), ())),
        preferred_element_type=jnp.float32,
    ).astype(jnp.bfloat16)
    received = lax.all_to_all(
        contributions, "ctx", 0, 0, tiled=True
    )
    update = jnp.sum(received.astype(jnp.float32), axis=0)
    scaled = weights[:, None] * update
    spread = jnp.dot(onehot.astype(jnp.float32).T, scaled, precision=HIGHEST_PRECISION)
    layer_out = (tokens[0].astype(jnp.float32) + spread).astype(jnp.bfloat16)[None]
    gate_back = jnp.sum(rows_back * update, axis=-1) * weights * (1.0 - weights)
    router_part = jnp.dot(gate_back, rows, precision=HIGHEST_PRECISION)
    router_split = jnp.stack(
        [
            router_part.astype(jnp.bfloat16),
            (router_part - router_part.astype(jnp.bfloat16).astype(jnp.float32)).astype(
                jnp.bfloat16
            ),
        ]
    )
    router_group = jnp.sum(
        lax.all_gather(router_split, "ctx", axis=0, tiled=False).astype(jnp.float32), axis=(0, 1)
    )
    router_high = router_group.astype(jnp.bfloat16)
    router_low = (router_group - router_high.astype(jnp.float32)).astype(jnp.bfloat16)
    factors = lax.all_gather(
        jnp.concatenate(
            [
                query_back,
                key_back,
                value_back,
            ],
            axis=0,
        ),
        "dp",
        axis=0,
        tiled=False,
    )

    def gathered(index):
        return factors[:, index * slots : (index + 1) * slots].reshape(n_dp * slots, inner)

    def contract(left, right):
        return lax.dot_general(
            left, right, (((0,), (0,)), ((), ())), preferred_element_type=jnp.float32
        ).astype(jnp.bfloat16)

    grad_query = contract(normed_blocks, gathered(0))
    grad_key = contract(normed_blocks, gathered(1))
    grad_value = contract(normed_blocks, gathered(2))
    dp_index = lax.axis_index("dp")
    delta_by_seq = delta_blocks.reshape(n_dp, slots, block)
    out_total = lax.dot_general(
        mixed,
        lax.dynamic_index_in_dim(delta_by_seq, dp_index, 0, keepdims=False),
        (((0,), (0,)), ((), ())),
        preferred_element_type=jnp.float32,
    )
    for shift in range(1, n_dp):
        arrived = lax.ppermute(mixed, "dp", [(i, (i + shift) % n_dp) for i in range(n_dp)])
        source = (dp_index + n_dp - shift) % n_dp
        out_total = out_total + lax.dot_general(
            arrived,
            lax.dynamic_index_in_dim(delta_by_seq, source, 0, keepdims=False),
            (((0,), (0,)), ((), ())),
            preferred_element_type=jnp.float32,
        )
    grad_out = out_total.astype(jnp.bfloat16)
    router_pieces = lax.all_gather(
        jnp.stack([router_high, router_low]), "dp", axis=0, tiled=False
    ).astype(jnp.float32)
    grad_router = jnp.sum(router_pieces[:, 0] + router_pieces[:, 1], axis=0)
    return (layer_out, grad_query, grad_key, grad_value, grad_out, grad_router)


def solution(mesh):
    n_dp = mesh.shape["dp"]
    n_ctx = mesh.shape["ctx"]
    in_specs = (
        P("dp", "ctx", None),
        P("dp", "ctx", None),
        P(),
        P(None, "ctx"),
        P(None, "ctx"),
        P(None, "ctx"),
        P("ctx", None),
        P("dp", "ctx"),
        P("dp", "ctx"),
    )
    out_specs = (
        P("dp", "ctx", None),
        P("dp", "ctx"),
        P("dp", "ctx"),
        P("dp", "ctx"),
        P("ctx", "dp"),
        P(),
    )

    def run(*args):
        return body(n_dp, n_ctx, *args)

    return jax.shard_map(run, mesh=mesh, in_specs=in_specs, out_specs=out_specs, check_vma=False)
```

```python
import math

import jax
import jax.numpy as jnp
from jax import lax
from jax.sharding import PartitionSpec as P

HDIM = 128


HIGHEST_PRECISION = lax.Precision.HIGHEST


def head_norm(values, width):
    shaped = values.reshape(values.shape[0], -1, width)
    inverse = lax.rsqrt(jnp.mean(shaped * shaped, axis=-1, keepdims=True) + 1e-06)
    return (shaped * inverse, inverse)


def norm_back(grad_hat, normal, inverse):
    return inverse * (grad_hat - normal * jnp.mean(grad_hat * normal, axis=-1, keepdims=True))


def rounded_term(part):
    return lax.optimization_barrier(part.astype(jnp.bfloat16)).astype(jnp.float32)


def body(n_dp, n_ctx, tokens, cotangent, w_router, w_query, w_key, w_value, w_out, chosen, counts):
    length = tokens.shape[1]
    width = tokens.shape[2]
    capacity = chosen.shape[1]
    inner = w_query.shape[1]
    heads_here = inner // HDIM
    scale = 1.0 / math.sqrt(HDIM)
    offset = lax.axis_index("ctx") * length
    slot_ids = lax.broadcasted_iota(jnp.int32, (capacity,), 0)
    local = chosen[0] - offset
    present = (slot_ids < counts[0, 0]) & (local >= 0) & (local < length)
    columns = lax.broadcasted_iota(jnp.int32, (capacity, length), 1)
    onehot = ((local[:, None] == columns) & present[:, None]).astype(jnp.bfloat16)
    rows = jnp.dot(onehot, tokens[0], preferred_element_type=jnp.float32)
    rows_back = jnp.dot(onehot, cotangent[0], preferred_element_type=jnp.float32)
    logits = jnp.dot(rows, w_router, precision=HIGHEST_PRECISION)
    weights = jax.nn.sigmoid(logits)
    normed = (rows * lax.rsqrt(jnp.mean(rows * rows, axis=-1, keepdims=True) + 1e-05)).astype(
        jnp.bfloat16
    )
    delta = (weights[:, None] * rows_back).astype(jnp.bfloat16)
    flag_cols = jnp.zeros((capacity, HDIM), jnp.bfloat16).at[:, 0].set(
        present.astype(jnp.bfloat16)
    )
    packed = lax.all_gather(
        jnp.concatenate([normed, delta, flag_cols], axis=1), "ctx", axis=0, tiled=False
    )
    chunk_normed = packed[:, :, :width]
    chunk_delta = packed[:, :, width : 2 * width]
    all_present = packed[:, :, 2 * width].reshape(n_ctx * capacity)
    slots = n_ctx * capacity
    block = width // n_dp
    own_blocks = lax.all_to_all(
        jnp.concatenate([normed, delta], axis=0), "dp", 1, 0, tiled=True
    )
    pieces = lax.all_gather(own_blocks, "ctx", axis=0, tiled=False).reshape(
        n_ctx, n_dp, 2, capacity, block
    )
    normed_blocks = pieces[:, :, 0].transpose(1, 0, 2, 3).reshape(n_dp * slots, block)
    delta_blocks = pieces[:, :, 1].transpose(1, 0, 2, 3).reshape(n_dp * slots, block)
    def project(weight):
        raw = lax.dot_general(
            chunk_normed, weight, (((2,), (0,)), ((), ())), preferred_element_type=jnp.float32
        )
        return raw.reshape(slots, inner)

    query_raw = project(w_query)
    key_raw = project(w_key)
    value_raw = project(w_value)
    query_hat, query_scale = head_norm(query_raw, HDIM)
    key_hat, key_scale = head_norm(key_raw, HDIM)
    query_b = query_hat.astype(jnp.bfloat16)
    key_b = key_hat.astype(jnp.bfloat16)
    value_b = value_raw.reshape(slots, heads_here, HDIM).astype(jnp.bfloat16)
    current = lax.broadcasted_iota(jnp.int32, (slots, slots), 0)
    earlier = lax.broadcasted_iota(jnp.int32, (slots, slots), 1)
    allowed = (earlier <= current) & ((all_present[None, :] > 0.5) | (earlier == current))
    scores = jnp.einsum("ihd,jhd->hij", query_b, key_b, preferred_element_type=jnp.float32) * scale
    exponent = jnp.where(allowed[None], jnp.exp(scores), 0.0)
    attend = exponent / jnp.sum(exponent, axis=-1, keepdims=True)
    attend_b = attend.astype(jnp.bfloat16)
    mixed = jnp.einsum("hij,jhd->ihd", attend_b, value_b, preferred_element_type=jnp.float32)
    mixed = mixed.astype(jnp.bfloat16).reshape(slots, inner)
    mixed_back = lax.dot_general(
        chunk_delta, w_out, (((2,), (1,)), ((), ())), preferred_element_type=jnp.float32
    )
    mixed_back = mixed_back.astype(jnp.bfloat16).reshape(slots, heads_here, HDIM)
    attend_back = jnp.einsum(
        "ihd,jhd->hij", mixed_back, value_b, preferred_element_type=jnp.float32
    )
    inner_sum = jnp.sum(attend * attend_back, axis=-1, keepdims=True)
    scores_back = (attend * (attend_back - inner_sum) * scale).astype(jnp.bfloat16)
    value_back = jnp.einsum(
        "hij,ihd->jhd", attend_b, mixed_back, preferred_element_type=jnp.float32
    )
    value_back = value_back.astype(jnp.bfloat16).reshape(slots, inner)
    qhat_back = jnp.einsum("hij,jhd->ihd", scores_back, key_b, preferred_element_type=jnp.float32)
    khat_back = jnp.einsum("hij,ihd->jhd", scores_back, query_b, preferred_element_type=jnp.float32)
    query_back = (
        norm_back(qhat_back, query_hat, query_scale).astype(jnp.bfloat16).reshape(slots, inner)
    )
    key_back = norm_back(khat_back, key_hat, key_scale).astype(jnp.bfloat16).reshape(slots, inner)
    mixed_late, query_back, key_back, value_back = lax.optimization_barrier(
        (mixed, query_back, key_back, value_back)
    )
    contributions = lax.dot_general(
        mixed_late.reshape(n_ctx, capacity, inner),
        w_out,
        (((2,), (0,)), ((), ())),
        preferred_element_type=jnp.float32,
    ).astype(jnp.bfloat16)
    received = lax.all_to_all(
        contributions, "ctx", 0, 0, tiled=True
    )
    update = jnp.sum(received.astype(jnp.float32), axis=0)
    scaled = weights[:, None] * update
    spread = jnp.dot(onehot.astype(jnp.float32).T, scaled, precision=HIGHEST_PRECISION)
    layer_out = (tokens[0].astype(jnp.float32) + spread).astype(jnp.bfloat16)[None]
    gate_back = jnp.sum(rows_back * update, axis=-1) * weights * (1.0 - weights)
    router_part = jnp.dot(gate_back, rows, precision=HIGHEST_PRECISION)
    router_split = jnp.stack(
        [
            router_part.astype(jnp.bfloat16),
            (router_part - router_part.astype(jnp.bfloat16).astype(jnp.float32)).astype(
                jnp.bfloat16
            ),
        ]
    )
    router_group = jnp.sum(
        lax.all_gather(router_split, "ctx", axis=0, tiled=False).astype(jnp.float32), axis=(0, 1)
    )
    router_high = router_group.astype(jnp.bfloat16)
    router_low = (router_group - router_high.astype(jnp.float32)).astype(jnp.bfloat16)
    factors = lax.all_gather(
        jnp.concatenate(
            [
                query_back,
                key_back,
                value_back,
            ],
            axis=0,
        ),
        "dp",
        axis=0,
        tiled=False,
    )

    def gathered(index):
        return factors[:, index * slots : (index + 1) * slots].reshape(n_dp * slots, inner)

    def contract(left, right):
        return lax.dot_general(
            left, right, (((0,), (0,)), ((), ())), preferred_element_type=jnp.float32
        ).astype(jnp.bfloat16)

    grad_query = contract(normed_blocks, gathered(0))
    grad_key = contract(normed_blocks, gathered(1))
    grad_value = contract(normed_blocks, gathered(2))
    dp_index = lax.axis_index("dp")
    delta_by_seq = delta_blocks.reshape(n_dp, slots, block)
    out_total = lax.dot_general(
        mixed,
        lax.dynamic_index_in_dim(delta_by_seq, dp_index, 0, keepdims=False),
        (((0,), (0,)), ((), ())),
        preferred_element_type=jnp.float32,
    )
    for shift in range(1, n_dp):
        arrived = lax.ppermute(mixed, "dp", [(i, (i + shift) % n_dp) for i in range(n_dp)])
        source = (dp_index + n_dp - shift) % n_dp
        out_total = out_total + lax.dot_general(
            arrived,
            lax.dynamic_index_in_dim(delta_by_seq, source, 0, keepdims=False),
            (((0,), (0,)), ((), ())),
            preferred_element_type=jnp.float32,
        )
    grad_out = out_total.astype(jnp.bfloat16)
    router_pair = jnp.stack([router_high, router_low])
    router_pieces = lax.dynamic_update_index_in_dim(
        jnp.zeros((n_dp,) + router_pair.shape, jnp.bfloat16), router_pair, dp_index, 0
    )
    for shift in range(1, n_dp):
        arrived = lax.ppermute(router_pair, "dp", [(i, (i + shift) % n_dp) for i in range(n_dp)])
        router_pieces = lax.dynamic_update_index_in_dim(
            router_pieces, arrived, (dp_index + n_dp - shift) % n_dp, 0
        )
    router_pieces = router_pieces.astype(jnp.float32)
    grad_router = jnp.sum(router_pieces[:, 0] + router_pieces[:, 1], axis=0)
    return (layer_out, grad_query, grad_key, grad_value, grad_out, grad_router)


def solution(mesh):
    n_dp = mesh.shape["dp"]
    n_ctx = mesh.shape["ctx"]
    in_specs = (
        P("dp", "ctx", None),
        P("dp", "ctx", None),
        P(),
        P(None, "ctx"),
        P(None, "ctx"),
        P(None, "ctx"),
        P("ctx", None),
        P("dp", "ctx"),
        P("dp", "ctx"),
    )
    out_specs = (
        P("dp", "ctx", None),
        P("dp", "ctx"),
        P("dp", "ctx"),
        P("dp", "ctx"),
        P("ctx", "dp"),
        P(),
    )

    def run(*args):
        return body(n_dp, n_ctx, *args)

    return jax.shard_map(run, mesh=mesh, in_specs=in_specs, out_specs=out_specs, check_vma=False)
```

```python
import math

import jax
import jax.numpy as jnp
from jax import lax
from jax.sharding import PartitionSpec as P

HDIM = 128


HIGHEST_PRECISION = lax.Precision.HIGHEST


def head_norm(values, width):
    shaped = values.reshape(values.shape[0], -1, width)
    inverse = lax.rsqrt(jnp.mean(shaped * shaped, axis=-1, keepdims=True) + 1e-06)
    return (shaped * inverse, inverse)


def norm_back(grad_hat, normal, inverse):
    return inverse * (grad_hat - normal * jnp.mean(grad_hat * normal, axis=-1, keepdims=True))


def rounded_term(part):
    return lax.optimization_barrier(part.astype(jnp.bfloat16)).astype(jnp.float32)


def body(n_dp, n_ctx, tokens, cotangent, w_router, w_query, w_key, w_value, w_out, chosen, counts):
    length = tokens.shape[1]
    width = tokens.shape[2]
    capacity = chosen.shape[1]
    inner = w_query.shape[1]
    heads_here = inner // HDIM
    scale = 1.0 / math.sqrt(HDIM)
    offset = lax.axis_index("ctx") * length
    slot_ids = lax.broadcasted_iota(jnp.int32, (capacity,), 0)
    local = chosen[0] - offset
    present = (slot_ids < counts[0, 0]) & (local >= 0) & (local < length)
    columns = lax.broadcasted_iota(jnp.int32, (capacity, length), 1)
    onehot = ((local[:, None] == columns) & present[:, None]).astype(jnp.bfloat16)
    rows = jnp.dot(onehot, tokens[0], preferred_element_type=jnp.float32)
    rows_back = jnp.dot(onehot, cotangent[0], preferred_element_type=jnp.float32)
    logits = jnp.dot(rows, w_router, precision=HIGHEST_PRECISION)
    weights = jax.nn.sigmoid(logits)
    normed = (rows * lax.rsqrt(jnp.mean(rows * rows, axis=-1, keepdims=True) + 1e-05)).astype(
        jnp.bfloat16
    )
    delta = (weights[:, None] * rows_back).astype(jnp.bfloat16)
    flag_cols = jnp.zeros((capacity, HDIM), jnp.bfloat16).at[:, 0].set(
        present.astype(jnp.bfloat16)
    )
    packed = lax.all_gather(
        jnp.concatenate([normed, delta, flag_cols], axis=1), "ctx", axis=0, tiled=False
    )
    chunk_normed = packed[:, :, :width]
    chunk_delta = packed[:, :, width : 2 * width]
    all_present = packed[:, :, 2 * width].reshape(n_ctx * capacity)
    slots = n_ctx * capacity
    block = width // n_dp
    own_blocks = lax.all_to_all(
        jnp.concatenate([normed, delta], axis=0), "dp", 1, 0, tiled=True
    )
    pieces = lax.all_gather(own_blocks, "ctx", axis=0, tiled=False).reshape(
        n_ctx, n_dp, 2, capacity, block
    )
    normed_blocks = pieces[:, :, 0].transpose(1, 0, 2, 3).reshape(n_dp * slots, block)
    delta_blocks = pieces[:, :, 1].transpose(1, 0, 2, 3).reshape(n_dp * slots, block)
    def project(weight):
        raw = lax.dot_general(
            chunk_normed, weight, (((2,), (0,)), ((), ())), preferred_element_type=jnp.float32
        )
        return raw.reshape(slots, inner)

    query_raw = project(w_query)
    key_raw = project(w_key)
    value_raw = project(w_value)
    query_hat, query_scale = head_norm(query_raw, HDIM)
    key_hat, key_scale = head_norm(key_raw, HDIM)
    query_b = query_hat.astype(jnp.bfloat16)
    key_b = key_hat.astype(jnp.bfloat16)
    value_b = value_raw.reshape(slots, heads_here, HDIM).astype(jnp.bfloat16)
    current = lax.broadcasted_iota(jnp.int32, (slots, slots), 0)
    earlier = lax.broadcasted_iota(jnp.int32, (slots, slots), 1)
    allowed = (earlier <= current) & ((all_present[None, :] > 0.5) | (earlier == current))
    scores = jnp.einsum("ihd,jhd->hij", query_b, key_b, preferred_element_type=jnp.float32) * scale
    exponent = jnp.where(allowed[None], jnp.exp(scores), 0.0)
    attend = exponent / jnp.sum(exponent, axis=-1, keepdims=True)
    attend_b = attend.astype(jnp.bfloat16)
    mixed = jnp.einsum("hij,jhd->ihd", attend_b, value_b, preferred_element_type=jnp.float32)
    mixed = mixed.astype(jnp.bfloat16).reshape(slots, inner)
    mixed_back = lax.dot_general(
        chunk_delta, w_out, (((2,), (1,)), ((), ())), preferred_element_type=jnp.float32
    )
    mixed_back = mixed_back.astype(jnp.bfloat16).reshape(slots, heads_here, HDIM)
    attend_back = jnp.einsum(
        "ihd,jhd->hij", mixed_back, value_b, preferred_element_type=jnp.float32
    )
    inner_sum = jnp.sum(attend * attend_back, axis=-1, keepdims=True)
    scores_back = (attend * (attend_back - inner_sum) * scale).astype(jnp.bfloat16)
    value_back = jnp.einsum(
        "hij,ihd->jhd", attend_b, mixed_back, preferred_element_type=jnp.float32
    )
    value_back = value_back.astype(jnp.bfloat16).reshape(slots, inner)
    qhat_back = jnp.einsum("hij,jhd->ihd", scores_back, key_b, preferred_element_type=jnp.float32)
    khat_back = jnp.einsum("hij,ihd->jhd", scores_back, query_b, preferred_element_type=jnp.float32)
    query_back = (
        norm_back(qhat_back, query_hat, query_scale).astype(jnp.bfloat16).reshape(slots, inner)
    )
    key_back = norm_back(khat_back, key_hat, key_scale).astype(jnp.bfloat16).reshape(slots, inner)
    mixed_late, query_back, key_back, value_back = lax.optimization_barrier(
        (mixed, query_back, key_back, value_back)
    )
    contributions = lax.dot_general(
        mixed_late.reshape(n_ctx, capacity, inner),
        w_out,
        (((2,), (0,)), ((), ())),
        preferred_element_type=jnp.float32,
    ).astype(jnp.bfloat16)
    received = lax.all_to_all(
        contributions, "ctx", 0, 0, tiled=True
    )
    update = jnp.sum(received.astype(jnp.float32), axis=0)
    scaled = weights[:, None] * update
    spread = jnp.dot(onehot.astype(jnp.float32).T, scaled, precision=HIGHEST_PRECISION)
    layer_out = (tokens[0].astype(jnp.float32) + spread).astype(jnp.bfloat16)[None]
    gate_back = jnp.sum(rows_back * update, axis=-1) * weights * (1.0 - weights)
    router_part = jnp.dot(gate_back, rows, precision=HIGHEST_PRECISION)
    router_split = jnp.stack(
        [
            router_part.astype(jnp.bfloat16),
            (router_part - router_part.astype(jnp.bfloat16).astype(jnp.float32)).astype(
                jnp.bfloat16
            ),
        ]
    )
    router_group = jnp.sum(
        lax.all_gather(router_split, "ctx", axis=0, tiled=False).astype(jnp.float32), axis=(0, 1)
    )
    router_high = router_group.astype(jnp.bfloat16)
    router_low = (router_group - router_high.astype(jnp.float32)).astype(jnp.bfloat16)
    factors = lax.all_gather(
        jnp.concatenate(
            [
                query_back,
                key_back,
                value_back,
            ],
            axis=0,
        ),
        "dp",
        axis=0,
        tiled=False,
    )

    def gathered(index):
        return factors[:, index * slots : (index + 1) * slots].reshape(n_dp * slots, inner)

    def contract(left, right):
        return lax.dot_general(
            left, right, (((0,), (0,)), ((), ())), preferred_element_type=jnp.float32
        ).astype(jnp.bfloat16)

    grad_query = contract(normed_blocks, gathered(0))
    grad_key = contract(normed_blocks, gathered(1))
    grad_value = contract(normed_blocks, gathered(2))
    dp_index = lax.axis_index("dp")
    mixed_by_source = lax.dynamic_update_index_in_dim(
        jnp.zeros((n_dp, slots, inner), jnp.bfloat16), mixed, dp_index, 0
    )
    for shift in range(1, n_dp):
        arrived = lax.ppermute(mixed, "dp", [(i, (i + shift) % n_dp) for i in range(n_dp)])
        mixed_by_source = lax.dynamic_update_index_in_dim(
            mixed_by_source, arrived, (dp_index + n_dp - shift) % n_dp, 0
        )
    grad_out = contract(mixed_by_source.reshape(n_dp * slots, inner), delta_blocks)
    router_pair = jnp.stack([router_high, router_low])
    router_pieces = lax.dynamic_update_index_in_dim(
        jnp.zeros((n_dp,) + router_pair.shape, jnp.bfloat16), router_pair, dp_index, 0
    )
    for shift in range(1, n_dp):
        arrived = lax.ppermute(router_pair, "dp", [(i, (i + shift) % n_dp) for i in range(n_dp)])
        router_pieces = lax.dynamic_update_index_in_dim(
            router_pieces, arrived, (dp_index + n_dp - shift) % n_dp, 0
        )
    router_pieces = router_pieces.astype(jnp.float32)
    grad_router = jnp.sum(router_pieces[:, 0] + router_pieces[:, 1], axis=0)
    return (layer_out, grad_query, grad_key, grad_value, grad_out, grad_router)


def solution(mesh):
    n_dp = mesh.shape["dp"]
    n_ctx = mesh.shape["ctx"]
    in_specs = (
        P("dp", "ctx", None),
        P("dp", "ctx", None),
        P(),
        P(None, "ctx"),
        P(None, "ctx"),
        P(None, "ctx"),
        P("ctx", None),
        P("dp", "ctx"),
        P("dp", "ctx"),
    )
    out_specs = (
        P("dp", "ctx", None),
        P("dp", "ctx"),
        P("dp", "ctx"),
        P("dp", "ctx"),
        P("ctx", "dp"),
        P(),
    )

    def run(*args):
        return body(n_dp, n_ctx, *args)

    return jax.shard_map(run, mesh=mesh, in_specs=in_specs, out_specs=out_specs, check_vma=False)
```

```python
import math

import jax
import jax.numpy as jnp
from jax import lax
from jax.sharding import PartitionSpec as P

HDIM = 128


HIGHEST_PRECISION = lax.Precision.HIGHEST


def head_norm(values, width):
    shaped = values.reshape(values.shape[0], -1, width)
    inverse = lax.rsqrt(jnp.mean(shaped * shaped, axis=-1, keepdims=True) + 1e-06)
    return (shaped * inverse, inverse)


def norm_back(grad_hat, normal, inverse):
    return inverse * (grad_hat - normal * jnp.mean(grad_hat * normal, axis=-1, keepdims=True))


def rounded_term(part):
    return lax.optimization_barrier(part.astype(jnp.bfloat16)).astype(jnp.float32)


def body(n_dp, n_ctx, tokens, cotangent, w_router, w_query, w_key, w_value, w_out, chosen, counts):
    length = tokens.shape[1]
    width = tokens.shape[2]
    capacity = chosen.shape[1]
    inner = w_query.shape[1]
    heads_here = inner // HDIM
    scale = 1.0 / math.sqrt(HDIM)
    offset = lax.axis_index("ctx") * length
    slot_ids = lax.broadcasted_iota(jnp.int32, (capacity,), 0)
    local = chosen[0] - offset
    present = (slot_ids < counts[0, 0]) & (local >= 0) & (local < length)
    columns = lax.broadcasted_iota(jnp.int32, (capacity, length), 1)
    onehot = ((local[:, None] == columns) & present[:, None]).astype(jnp.bfloat16)
    rows = jnp.dot(onehot, tokens[0], preferred_element_type=jnp.float32)
    rows_back = jnp.dot(onehot, cotangent[0], preferred_element_type=jnp.float32)
    logits = jnp.dot(rows, w_router, precision=HIGHEST_PRECISION)
    weights = jax.nn.sigmoid(logits)
    normed = (rows * lax.rsqrt(jnp.mean(rows * rows, axis=-1, keepdims=True) + 1e-05)).astype(
        jnp.bfloat16
    )
    delta = (weights[:, None] * rows_back).astype(jnp.bfloat16)
    flag_cols = jnp.zeros((capacity, HDIM), jnp.bfloat16).at[:, 0].set(
        present.astype(jnp.bfloat16)
    )
    packed = lax.all_gather(
        jnp.concatenate([normed, delta, flag_cols], axis=1), "ctx", axis=0, tiled=False
    )
    chunk_normed = packed[:, :, :width]
    chunk_delta = packed[:, :, width : 2 * width]
    all_present = packed[:, :, 2 * width].reshape(n_ctx * capacity)
    slots = n_ctx * capacity
    block = width // n_dp
    own_blocks = lax.all_to_all(
        jnp.concatenate([normed, delta], axis=0), "dp", 1, 0, tiled=True
    )
    pieces = lax.all_gather(own_blocks, "ctx", axis=0, tiled=False).reshape(
        n_ctx, n_dp, 2, capacity, block
    )
    normed_blocks = pieces[:, :, 0].transpose(1, 0, 2, 3).reshape(n_dp * slots, block)
    delta_blocks = pieces[:, :, 1].transpose(1, 0, 2, 3).reshape(n_dp * slots, block)
    def project(weight):
        raw = lax.dot_general(
            chunk_normed, weight, (((2,), (0,)), ((), ())), preferred_element_type=jnp.float32
        )
        return raw.reshape(slots, inner)

    query_raw = project(w_query)
    key_raw = project(w_key)
    value_raw = project(w_value)
    query_hat, query_scale = head_norm(query_raw, HDIM)
    key_hat, key_scale = head_norm(key_raw, HDIM)
    query_b = query_hat.astype(jnp.bfloat16)
    key_b = key_hat.astype(jnp.bfloat16)
    value_b = value_raw.reshape(slots, heads_here, HDIM).astype(jnp.bfloat16)
    current = lax.broadcasted_iota(jnp.int32, (slots, slots), 0)
    earlier = lax.broadcasted_iota(jnp.int32, (slots, slots), 1)
    allowed = (earlier <= current) & ((all_present[None, :] > 0.5) | (earlier == current))
    scores = jnp.einsum("ihd,jhd->hij", query_b, key_b, preferred_element_type=jnp.float32) * scale
    exponent = jnp.where(allowed[None], jnp.exp(scores), 0.0)
    attend = exponent / jnp.sum(exponent, axis=-1, keepdims=True)
    attend_b = attend.astype(jnp.bfloat16)
    mixed = jnp.einsum("hij,jhd->ihd", attend_b, value_b, preferred_element_type=jnp.float32)
    mixed = mixed.astype(jnp.bfloat16).reshape(slots, inner)
    mixed_back = lax.dot_general(
        chunk_delta, w_out, (((2,), (1,)), ((), ())), preferred_element_type=jnp.float32
    )
    mixed_back = mixed_back.astype(jnp.bfloat16).reshape(slots, heads_here, HDIM)
    attend_back = jnp.einsum(
        "ihd,jhd->hij", mixed_back, value_b, preferred_element_type=jnp.float32
    )
    inner_sum = jnp.sum(attend * attend_back, axis=-1, keepdims=True)
    scores_back = (attend * (attend_back - inner_sum) * scale).astype(jnp.bfloat16)
    value_back = jnp.einsum(
        "hij,ihd->jhd", attend_b, mixed_back, preferred_element_type=jnp.float32
    )
    value_back = value_back.astype(jnp.bfloat16).reshape(slots, inner)
    qhat_back = jnp.einsum("hij,jhd->ihd", scores_back, key_b, preferred_element_type=jnp.float32)
    khat_back = jnp.einsum("hij,ihd->jhd", scores_back, query_b, preferred_element_type=jnp.float32)
    query_back = (
        norm_back(qhat_back, query_hat, query_scale).astype(jnp.bfloat16).reshape(slots, inner)
    )
    key_back = norm_back(khat_back, key_hat, key_scale).astype(jnp.bfloat16).reshape(slots, inner)
    mixed_late, query_back, key_back, value_back = lax.optimization_barrier(
        (mixed, query_back, key_back, value_back)
    )
    contributions = lax.dot_general(
        mixed_late.reshape(n_ctx, capacity, inner),
        w_out,
        (((2,), (0,)), ((), ())),
        preferred_element_type=jnp.float32,
    ).astype(jnp.bfloat16)
    received = lax.all_to_all(
        contributions, "ctx", 0, 0, tiled=True
    )
    update = jnp.sum(received.astype(jnp.float32), axis=0)
    scaled = weights[:, None] * update
    spread = jnp.dot(onehot.astype(jnp.float32).T, scaled, precision=HIGHEST_PRECISION)
    layer_out = (tokens[0].astype(jnp.float32) + spread).astype(jnp.bfloat16)[None]
    gate_back = jnp.sum(rows_back * update, axis=-1) * weights * (1.0 - weights)
    router_part = jnp.dot(gate_back, rows, precision=HIGHEST_PRECISION)
    router_split = jnp.stack(
        [
            router_part.astype(jnp.bfloat16),
            (router_part - router_part.astype(jnp.bfloat16).astype(jnp.float32)).astype(
                jnp.bfloat16
            ),
        ]
    )
    router_group = jnp.sum(
        lax.all_gather(router_split, "ctx", axis=0, tiled=False).astype(jnp.float32), axis=(0, 1)
    )
    router_high = router_group.astype(jnp.bfloat16)
    router_low = (router_group - router_high.astype(jnp.float32)).astype(jnp.bfloat16)
    factors = lax.all_gather(
        jnp.concatenate(
            [
                query_back,
                key_back,
            ],
            axis=0,
        ),
        "dp",
        axis=0,
        tiled=False,
    )

    def gathered(index):
        return factors[:, index * slots : (index + 1) * slots].reshape(n_dp * slots, inner)

    def contract(left, right):
        return lax.dot_general(
            left, right, (((0,), (0,)), ((), ())), preferred_element_type=jnp.float32
        ).astype(jnp.bfloat16)

    grad_query = contract(normed_blocks, gathered(0))
    grad_key = contract(normed_blocks, gathered(1))
    dp_index = lax.axis_index("dp")
    delta_by_seq = delta_blocks.reshape(n_dp, slots, block)
    out_total = lax.dot_general(
        mixed,
        lax.dynamic_index_in_dim(delta_by_seq, dp_index, 0, keepdims=False),
        (((0,), (0,)), ((), ())),
        preferred_element_type=jnp.float32,
    )
    for shift in range(1, n_dp):
        arrived = lax.ppermute(mixed, "dp", [(i, (i + shift) % n_dp) for i in range(n_dp)])
        source = (dp_index + n_dp - shift) % n_dp
        out_total = out_total + lax.dot_general(
            arrived,
            lax.dynamic_index_in_dim(delta_by_seq, source, 0, keepdims=False),
            (((0,), (0,)), ((), ())),
            preferred_element_type=jnp.float32,
        )
    grad_out = out_total.astype(jnp.bfloat16)
    value_by_source = lax.dynamic_update_index_in_dim(
        jnp.zeros((n_dp, slots, inner), jnp.bfloat16), value_back, dp_index, 0
    )
    for shift in range(1, n_dp):
        arrived = lax.ppermute(value_back, "dp", [(i, (i + shift) % n_dp) for i in range(n_dp)])
        value_by_source = lax.dynamic_update_index_in_dim(
            value_by_source, arrived, (dp_index + n_dp - shift) % n_dp, 0
        )
    grad_value = contract(normed_blocks, value_by_source.reshape(n_dp * slots, inner))
    router_pair = jnp.stack([router_high, router_low])
    router_pieces = lax.dynamic_update_index_in_dim(
        jnp.zeros((n_dp,) + router_pair.shape, jnp.bfloat16), router_pair, dp_index, 0
    )
    for shift in range(1, n_dp):
        arrived = lax.ppermute(router_pair, "dp", [(i, (i + shift) % n_dp) for i in range(n_dp)])
        router_pieces = lax.dynamic_update_index_in_dim(
            router_pieces, arrived, (dp_index + n_dp - shift) % n_dp, 0
        )
    router_pieces = router_pieces.astype(jnp.float32)
    grad_router = jnp.sum(router_pieces[:, 0] + router_pieces[:, 1], axis=0)
    return (layer_out, grad_query, grad_key, grad_value, grad_out, grad_router)


def solution(mesh):
    n_dp = mesh.shape["dp"]
    n_ctx = mesh.shape["ctx"]
    in_specs = (
        P("dp", "ctx", None),
        P("dp", "ctx", None),
        P(),
        P(None, "ctx"),
        P(None, "ctx"),
        P(None, "ctx"),
        P("ctx", None),
        P("dp", "ctx"),
        P("dp", "ctx"),
    )
    out_specs = (
        P("dp", "ctx", None),
        P("dp", "ctx"),
        P("dp", "ctx"),
        P("dp", "ctx"),
        P("ctx", "dp"),
        P(),
    )

    def run(*args):
        return body(n_dp, n_ctx, *args)

    return jax.shard_map(run, mesh=mesh, in_specs=in_specs, out_specs=out_specs, check_vma=False)
```

```python
import math

import jax
import jax.numpy as jnp
from jax import lax
from jax.sharding import PartitionSpec as P

HDIM = 128


HIGHEST_PRECISION = lax.Precision.HIGHEST


def head_norm(values, width):
    shaped = values.reshape(values.shape[0], -1, width)
    inverse = lax.rsqrt(jnp.mean(shaped * shaped, axis=-1, keepdims=True) + 1e-06)
    return (shaped * inverse, inverse)


def norm_back(grad_hat, normal, inverse):
    return inverse * (grad_hat - normal * jnp.mean(grad_hat * normal, axis=-1, keepdims=True))


def rounded_term(part):
    return lax.optimization_barrier(part.astype(jnp.bfloat16)).astype(jnp.float32)


def body(n_dp, n_ctx, tokens, cotangent, w_router, w_query, w_key, w_value, w_out, chosen, counts):
    length = tokens.shape[1]
    width = tokens.shape[2]
    capacity = chosen.shape[1]
    inner = w_query.shape[1]
    heads_here = inner // HDIM
    scale = 1.0 / math.sqrt(HDIM)
    offset = lax.axis_index("ctx") * length
    slot_ids = lax.broadcasted_iota(jnp.int32, (capacity,), 0)
    local = chosen[0] - offset
    present = (slot_ids < counts[0, 0]) & (local >= 0) & (local < length)
    columns = lax.broadcasted_iota(jnp.int32, (capacity, length), 1)
    onehot = ((local[:, None] == columns) & present[:, None]).astype(jnp.bfloat16)
    rows = jnp.dot(onehot, tokens[0], preferred_element_type=jnp.float32)
    rows_back = jnp.dot(onehot, cotangent[0], preferred_element_type=jnp.float32)
    logits = jnp.dot(rows, w_router, precision=HIGHEST_PRECISION)
    weights = jax.nn.sigmoid(logits)
    normed = (rows * lax.rsqrt(jnp.mean(rows * rows, axis=-1, keepdims=True) + 1e-05)).astype(
        jnp.bfloat16
    )
    delta = (weights[:, None] * rows_back).astype(jnp.bfloat16)
    flag_cols = jnp.zeros((capacity, HDIM), jnp.bfloat16).at[:, 0].set(
        present.astype(jnp.bfloat16)
    )
    packed = lax.all_gather(
        jnp.concatenate([normed, delta, flag_cols], axis=1), "ctx", axis=0, tiled=False
    )
    chunk_normed = packed[:, :, :width]
    chunk_delta = packed[:, :, width : 2 * width]
    all_present = packed[:, :, 2 * width].reshape(n_ctx * capacity)
    slots = n_ctx * capacity
    block = width // n_dp
    own_blocks = lax.all_to_all(
        jnp.concatenate([normed, delta], axis=0), "dp", 1, 0, tiled=True
    )
    pieces = lax.all_gather(own_blocks, "ctx", axis=0, tiled=False).reshape(
        n_ctx, n_dp, 2, capacity, block
    )
    normed_blocks = pieces[:, :, 0].transpose(1, 0, 2, 3).reshape(n_dp * slots, block)
    delta_blocks = pieces[:, :, 1].transpose(1, 0, 2, 3).reshape(n_dp * slots, block)
    def project(weight):
        raw = lax.dot_general(
            chunk_normed, weight, (((2,), (0,)), ((), ())), preferred_element_type=jnp.float32
        )
        return raw.reshape(slots, inner)

    query_raw = project(w_query)
    key_raw = project(w_key)
    value_raw = project(w_value)
    query_hat, query_scale = head_norm(query_raw, HDIM)
    key_hat, key_scale = head_norm(key_raw, HDIM)
    query_b = query_hat.astype(jnp.bfloat16)
    key_b = key_hat.astype(jnp.bfloat16)
    value_b = value_raw.reshape(slots, heads_here, HDIM).astype(jnp.bfloat16)
    current = lax.broadcasted_iota(jnp.int32, (slots, slots), 0)
    earlier = lax.broadcasted_iota(jnp.int32, (slots, slots), 1)
    allowed = (earlier <= current) & ((all_present[None, :] > 0.5) | (earlier == current))
    scores = jnp.einsum("ihd,jhd->hij", query_b, key_b, preferred_element_type=jnp.float32) * scale
    exponent = jnp.where(allowed[None], jnp.exp(scores), 0.0)
    attend = exponent / jnp.sum(exponent, axis=-1, keepdims=True)
    attend_b = attend.astype(jnp.bfloat16)
    mixed = jnp.einsum("hij,jhd->ihd", attend_b, value_b, preferred_element_type=jnp.float32)
    mixed = mixed.astype(jnp.bfloat16).reshape(slots, inner)
    mixed_back = lax.dot_general(
        chunk_delta, w_out, (((2,), (1,)), ((), ())), preferred_element_type=jnp.float32
    )
    mixed_back = mixed_back.astype(jnp.bfloat16).reshape(slots, heads_here, HDIM)
    attend_back = jnp.einsum(
        "ihd,jhd->hij", mixed_back, value_b, preferred_element_type=jnp.float32
    )
    inner_sum = jnp.sum(attend * attend_back, axis=-1, keepdims=True)
    scores_back = (attend * (attend_back - inner_sum) * scale).astype(jnp.bfloat16)
    value_back = jnp.einsum(
        "hij,ihd->jhd", attend_b, mixed_back, preferred_element_type=jnp.float32
    )
    value_back = value_back.astype(jnp.bfloat16).reshape(slots, inner)
    qhat_back = jnp.einsum("hij,jhd->ihd", scores_back, key_b, preferred_element_type=jnp.float32)
    khat_back = jnp.einsum("hij,ihd->jhd", scores_back, query_b, preferred_element_type=jnp.float32)
    query_back = (
        norm_back(qhat_back, query_hat, query_scale).astype(jnp.bfloat16).reshape(slots, inner)
    )
    key_back = norm_back(khat_back, key_hat, key_scale).astype(jnp.bfloat16).reshape(slots, inner)
    mixed_late, query_back, key_back, value_back = lax.optimization_barrier(
        (mixed, query_back, key_back, value_back)
    )
    contributions = lax.dot_general(
        mixed_late.reshape(n_ctx, capacity, inner),
        w_out,
        (((2,), (0,)), ((), ())),
        preferred_element_type=jnp.float32,
    ).astype(jnp.bfloat16)
    received = lax.all_to_all(
        contributions, "ctx", 0, 0, tiled=True
    )
    update = jnp.sum(received.astype(jnp.float32), axis=0)
    scaled = weights[:, None] * update
    spread = jnp.dot(onehot.astype(jnp.float32).T, scaled, precision=HIGHEST_PRECISION)
    layer_out = (tokens[0].astype(jnp.float32) + spread).astype(jnp.bfloat16)[None]
    gate_back = jnp.sum(rows_back * update, axis=-1) * weights * (1.0 - weights)
    router_part = jnp.dot(gate_back, rows, precision=HIGHEST_PRECISION)
    router_split = jnp.stack(
        [
            router_part.astype(jnp.bfloat16),
            (router_part - router_part.astype(jnp.bfloat16).astype(jnp.float32)).astype(
                jnp.bfloat16
            ),
        ]
    )
    router_group = jnp.sum(
        lax.all_gather(router_split, "ctx", axis=0, tiled=False).astype(jnp.float32), axis=(0, 1)
    )
    factors = lax.all_gather(
        jnp.concatenate(
            [
                query_back,
                key_back,
                value_back,
            ],
            axis=0,
        ),
        "dp",
        axis=0,
        tiled=False,
    )

    def gathered(index):
        return factors[:, index * slots : (index + 1) * slots].reshape(n_dp * slots, inner)

    def contract(left, right):
        return lax.dot_general(
            left, right, (((0,), (0,)), ((), ())), preferred_element_type=jnp.float32
        ).astype(jnp.bfloat16)

    grad_query = contract(normed_blocks, gathered(0))
    grad_key = contract(normed_blocks, gathered(1))
    grad_value = contract(normed_blocks, gathered(2))
    dp_index = lax.axis_index("dp")
    delta_by_seq = delta_blocks.reshape(n_dp, slots, block)
    out_total = lax.dot_general(
        mixed,
        lax.dynamic_index_in_dim(delta_by_seq, dp_index, 0, keepdims=False),
        (((0,), (0,)), ((), ())),
        preferred_element_type=jnp.float32,
    )
    for shift in range(1, n_dp):
        arrived = lax.ppermute(mixed, "dp", [(i, (i + shift) % n_dp) for i in range(n_dp)])
        source = (dp_index + n_dp - shift) % n_dp
        out_total = out_total + lax.dot_general(
            arrived,
            lax.dynamic_index_in_dim(delta_by_seq, source, 0, keepdims=False),
            (((0,), (0,)), ((), ())),
            preferred_element_type=jnp.float32,
        )
    grad_out = out_total.astype(jnp.bfloat16)
    grad_router = router_group
    bit = 1
    while bit < n_dp:
        grad_router = grad_router + lax.ppermute(
            grad_router, "dp", [(i, i ^ bit) for i in range(n_dp)]
        )
        bit *= 2
    return (layer_out, grad_query, grad_key, grad_value, grad_out, grad_router)


def solution(mesh):
    n_dp = mesh.shape["dp"]
    n_ctx = mesh.shape["ctx"]
    in_specs = (
        P("dp", "ctx", None),
        P("dp", "ctx", None),
        P(),
        P(None, "ctx"),
        P(None, "ctx"),
        P(None, "ctx"),
        P("ctx", None),
        P("dp", "ctx"),
        P("dp", "ctx"),
    )
    out_specs = (
        P("dp", "ctx", None),
        P("dp", "ctx"),
        P("dp", "ctx"),
        P("dp", "ctx"),
        P("ctx", "dp"),
        P(),
    )

    def run(*args):
        return body(n_dp, n_ctx, *args)

    return jax.shard_map(run, mesh=mesh, in_specs=in_specs, out_specs=out_specs, check_vma=False)
```

```python
import math

import jax
import jax.numpy as jnp
from jax import lax
from jax.sharding import PartitionSpec as P

HDIM = 128


HIGHEST_PRECISION = lax.Precision.HIGHEST


def head_norm(values, width):
    shaped = values.reshape(values.shape[0], -1, width)
    inverse = lax.rsqrt(jnp.mean(shaped * shaped, axis=-1, keepdims=True) + 1e-06)
    return (shaped * inverse, inverse)


def norm_back(grad_hat, normal, inverse):
    return inverse * (grad_hat - normal * jnp.mean(grad_hat * normal, axis=-1, keepdims=True))


def rounded_term(part):
    return lax.optimization_barrier(part.astype(jnp.bfloat16)).astype(jnp.float32)


def body(n_dp, n_ctx, tokens, cotangent, w_router, w_query, w_key, w_value, w_out, chosen, counts):
    length = tokens.shape[1]
    width = tokens.shape[2]
    capacity = chosen.shape[1]
    inner = w_query.shape[1]
    heads_here = inner // HDIM
    scale = 1.0 / math.sqrt(HDIM)
    offset = lax.axis_index("ctx") * length
    slot_ids = lax.broadcasted_iota(jnp.int32, (capacity,), 0)
    local = chosen[0] - offset
    present = (slot_ids < counts[0, 0]) & (local >= 0) & (local < length)
    columns = lax.broadcasted_iota(jnp.int32, (capacity, length), 1)
    onehot = ((local[:, None] == columns) & present[:, None]).astype(jnp.bfloat16)
    rows = jnp.dot(onehot, tokens[0], preferred_element_type=jnp.float32)
    rows_back = jnp.dot(onehot, cotangent[0], preferred_element_type=jnp.float32)
    logits = jnp.dot(rows, w_router, precision=HIGHEST_PRECISION)
    weights = jax.nn.sigmoid(logits)
    normed = (rows * lax.rsqrt(jnp.mean(rows * rows, axis=-1, keepdims=True) + 1e-05)).astype(
        jnp.bfloat16
    )
    delta = (weights[:, None] * rows_back).astype(jnp.bfloat16)
    flag_cols = jnp.zeros((capacity, HDIM), jnp.bfloat16).at[:, 0].set(
        present.astype(jnp.bfloat16)
    )
    packed = lax.all_gather(
        jnp.concatenate([normed, delta, flag_cols], axis=1), "ctx", axis=0, tiled=False
    )
    chunk_normed = packed[:, :, :width]
    chunk_delta = packed[:, :, width : 2 * width]
    all_present = packed[:, :, 2 * width].reshape(n_ctx * capacity)
    slots = n_ctx * capacity
    block = width // n_dp
    own_blocks = lax.all_to_all(
        jnp.concatenate([normed, delta], axis=0), "dp", 1, 0, tiled=True
    )
    pieces = lax.all_gather(own_blocks, "ctx", axis=0, tiled=False).reshape(
        n_ctx, n_dp, 2, capacity, block
    )
    normed_blocks = pieces[:, :, 0].transpose(1, 0, 2, 3).reshape(n_dp * slots, block)
    delta_blocks = pieces[:, :, 1].transpose(1, 0, 2, 3).reshape(n_dp * slots, block)
    def project(weight):
        raw = lax.dot_general(
            chunk_normed, weight, (((2,), (0,)), ((), ())), preferred_element_type=jnp.float32
        )
        return raw.reshape(slots, inner)

    query_raw = project(w_query)
    key_raw = project(w_key)
    value_raw = project(w_value)
    query_hat, query_scale = head_norm(query_raw, HDIM)
    key_hat, key_scale = head_norm(key_raw, HDIM)
    query_b = query_hat.astype(jnp.bfloat16)
    key_b = key_hat.astype(jnp.bfloat16)
    value_b = value_raw.reshape(slots, heads_here, HDIM).astype(jnp.bfloat16)
    current = lax.broadcasted_iota(jnp.int32, (slots, slots), 0)
    earlier = lax.broadcasted_iota(jnp.int32, (slots, slots), 1)
    allowed = (earlier <= current) & ((all_present[None, :] > 0.5) | (earlier == current))
    scores = jnp.einsum("ihd,jhd->hij", query_b, key_b, preferred_element_type=jnp.float32) * scale
    exponent = jnp.where(allowed[None], jnp.exp(scores), 0.0)
    attend = exponent / jnp.sum(exponent, axis=-1, keepdims=True)
    attend_b = attend.astype(jnp.bfloat16)
    mixed = jnp.einsum("hij,jhd->ihd", attend_b, value_b, preferred_element_type=jnp.float32)
    mixed = mixed.astype(jnp.bfloat16).reshape(slots, inner)
    mixed_back = lax.dot_general(
        chunk_delta, w_out, (((2,), (1,)), ((), ())), preferred_element_type=jnp.float32
    )
    mixed_back = mixed_back.astype(jnp.bfloat16).reshape(slots, heads_here, HDIM)
    attend_back = jnp.einsum(
        "ihd,jhd->hij", mixed_back, value_b, preferred_element_type=jnp.float32
    )
    inner_sum = jnp.sum(attend * attend_back, axis=-1, keepdims=True)
    scores_back = (attend * (attend_back - inner_sum) * scale).astype(jnp.bfloat16)
    value_back = jnp.einsum(
        "hij,ihd->jhd", attend_b, mixed_back, preferred_element_type=jnp.float32
    )
    value_back = value_back.astype(jnp.bfloat16).reshape(slots, inner)
    qhat_back = jnp.einsum("hij,jhd->ihd", scores_back, key_b, preferred_element_type=jnp.float32)
    khat_back = jnp.einsum("hij,ihd->jhd", scores_back, query_b, preferred_element_type=jnp.float32)
    query_back = (
        norm_back(qhat_back, query_hat, query_scale).astype(jnp.bfloat16).reshape(slots, inner)
    )
    key_back = norm_back(khat_back, key_hat, key_scale).astype(jnp.bfloat16).reshape(slots, inner)
    mixed_late, query_back, key_back, value_back = lax.optimization_barrier(
        (mixed, query_back, key_back, value_back)
    )
    contributions = lax.dot_general(
        mixed_late.reshape(n_ctx, capacity, inner),
        w_out,
        (((2,), (0,)), ((), ())),
        preferred_element_type=jnp.float32,
    ).astype(jnp.bfloat16)
    received = lax.all_to_all(
        contributions, "ctx", 0, 0, tiled=True
    )
    update = jnp.sum(received.astype(jnp.float32), axis=0)
    scaled = weights[:, None] * update
    spread = jnp.dot(onehot.astype(jnp.float32).T, scaled, precision=HIGHEST_PRECISION)
    layer_out = (tokens[0].astype(jnp.float32) + spread).astype(jnp.bfloat16)[None]
    gate_back = jnp.sum(rows_back * update, axis=-1) * weights * (1.0 - weights)
    router_part = jnp.dot(gate_back, rows, precision=HIGHEST_PRECISION)
    router_split = jnp.stack(
        [
            router_part.astype(jnp.bfloat16),
            (router_part - router_part.astype(jnp.bfloat16).astype(jnp.float32)).astype(
                jnp.bfloat16
            ),
        ]
    )
    router_group = jnp.sum(
        lax.all_gather(router_split, "ctx", axis=0, tiled=False).astype(jnp.float32), axis=(0, 1)
    )
    router_high = router_group.astype(jnp.bfloat16)
    router_low = (router_group - router_high.astype(jnp.float32)).astype(jnp.bfloat16)
    factors = lax.all_gather(
        jnp.concatenate([query_back, key_back, value_back], axis=1), "dp", axis=0, tiled=False
    ).reshape(n_dp * slots, 3 * inner)

    def contract(left, right):
        return lax.dot_general(
            left, right, (((0,), (0,)), ((), ())), preferred_element_type=jnp.float32
        ).astype(jnp.bfloat16)

    grads = contract(normed_blocks, factors)
    grad_query = grads[:, :inner]
    grad_key = grads[:, inner : 2 * inner]
    grad_value = grads[:, 2 * inner :]
    dp_index = lax.axis_index("dp")
    delta_by_seq = delta_blocks.reshape(n_dp, slots, block)
    out_total = lax.dot_general(
        mixed,
        lax.dynamic_index_in_dim(delta_by_seq, dp_index, 0, keepdims=False),
        (((0,), (0,)), ((), ())),
        preferred_element_type=jnp.float32,
    )
    for shift in range(1, n_dp):
        arrived = lax.ppermute(mixed, "dp", [(i, (i + shift) % n_dp) for i in range(n_dp)])
        source = (dp_index + n_dp - shift) % n_dp
        out_total = out_total + lax.dot_general(
            arrived,
            lax.dynamic_index_in_dim(delta_by_seq, source, 0, keepdims=False),
            (((0,), (0,)), ((), ())),
            preferred_element_type=jnp.float32,
        )
    grad_out = out_total.astype(jnp.bfloat16)
    router_pair = jnp.stack([router_high, router_low])
    router_pieces = lax.dynamic_update_index_in_dim(
        jnp.zeros((n_dp,) + router_pair.shape, jnp.bfloat16), router_pair, dp_index, 0
    )
    for shift in range(1, n_dp):
        arrived = lax.ppermute(router_pair, "dp", [(i, (i + shift) % n_dp) for i in range(n_dp)])
        router_pieces = lax.dynamic_update_index_in_dim(
            router_pieces, arrived, (dp_index + n_dp - shift) % n_dp, 0
        )
    router_pieces = router_pieces.astype(jnp.float32)
    grad_router = jnp.sum(router_pieces[:, 0] + router_pieces[:, 1], axis=0)
    return (layer_out, grad_query, grad_key, grad_value, grad_out, grad_router)


def solution(mesh):
    n_dp = mesh.shape["dp"]
    n_ctx = mesh.shape["ctx"]
    in_specs = (
        P("dp", "ctx", None),
        P("dp", "ctx", None),
        P(),
        P(None, "ctx"),
        P(None, "ctx"),
        P(None, "ctx"),
        P("ctx", None),
        P("dp", "ctx"),
        P("dp", "ctx"),
    )
    out_specs = (
        P("dp", "ctx", None),
        P("dp", "ctx"),
        P("dp", "ctx"),
        P("dp", "ctx"),
        P("ctx", "dp"),
        P(),
    )

    def run(*args):
        return body(n_dp, n_ctx, *args)

    return jax.shard_map(run, mesh=mesh, in_specs=in_specs, out_specs=out_specs, check_vma=False)
```

```python
import math

import jax
import jax.numpy as jnp
from jax import lax
from jax.sharding import PartitionSpec as P

HDIM = 128


HIGHEST_PRECISION = lax.Precision.HIGHEST


def head_norm(values, width):
    shaped = values.reshape(values.shape[0], -1, width)
    inverse = lax.rsqrt(jnp.mean(shaped * shaped, axis=-1, keepdims=True) + 1e-06)
    return (shaped * inverse, inverse)


def norm_back(grad_hat, normal, inverse):
    return inverse * (grad_hat - normal * jnp.mean(grad_hat * normal, axis=-1, keepdims=True))


def bf16_pieces(values):
    high = values.astype(jnp.bfloat16)
    rest = values - high.astype(jnp.float32)
    middle = rest.astype(jnp.bfloat16)
    low = (rest - middle.astype(jnp.float32)).astype(jnp.bfloat16)
    return jnp.stack([high, middle, low])


def rounded_term(part):
    return lax.optimization_barrier(part.astype(jnp.bfloat16)).astype(jnp.float32)


def body(n_dp, n_ctx, tokens, cotangent, w_router, w_query, w_key, w_value, w_out, chosen, counts):
    length = tokens.shape[1]
    width = tokens.shape[2]
    capacity = chosen.shape[1]
    inner = w_query.shape[1]
    heads_here = inner // HDIM
    scale = 1.0 / math.sqrt(HDIM)
    offset = lax.axis_index("ctx") * length
    slot_ids = lax.broadcasted_iota(jnp.int32, (capacity,), 0)
    local = chosen[0] - offset
    present = (slot_ids < counts[0, 0]) & (local >= 0) & (local < length)
    columns = lax.broadcasted_iota(jnp.int32, (capacity, length), 1)
    onehot = ((local[:, None] == columns) & present[:, None]).astype(jnp.bfloat16)
    rows = jnp.dot(onehot, tokens[0], preferred_element_type=jnp.float32)
    rows_back = jnp.dot(onehot, cotangent[0], preferred_element_type=jnp.float32)
    logits = jnp.dot(rows, w_router, precision=HIGHEST_PRECISION)
    weights = jax.nn.sigmoid(logits)
    normed = (rows * lax.rsqrt(jnp.mean(rows * rows, axis=-1, keepdims=True) + 1e-05)).astype(
        jnp.bfloat16
    )
    delta = (weights[:, None] * rows_back).astype(jnp.bfloat16)
    flag_cols = jnp.zeros((capacity, HDIM), jnp.bfloat16).at[:, 0].set(
        present.astype(jnp.bfloat16)
    )
    packed = lax.all_gather(
        jnp.concatenate([normed, delta, flag_cols], axis=1), "ctx", axis=0, tiled=False
    )
    chunk_normed = packed[:, :, :width]
    chunk_delta = packed[:, :, width : 2 * width]
    all_present = packed[:, :, 2 * width].reshape(n_ctx * capacity)
    slots = n_ctx * capacity
    block = width // n_dp
    own_blocks = lax.all_to_all(
        jnp.concatenate([normed, delta], axis=0), "dp", 1, 0, tiled=True
    )
    pieces = lax.all_gather(own_blocks, "ctx", axis=0, tiled=False).reshape(
        n_ctx, n_dp, 2, capacity, block
    )
    normed_blocks = pieces[:, :, 0].transpose(1, 0, 2, 3).reshape(n_dp * slots, block)
    delta_blocks = pieces[:, :, 1].transpose(1, 0, 2, 3).reshape(n_dp * slots, block)
    def project(weight):
        raw = lax.dot_general(
            chunk_normed, weight, (((2,), (0,)), ((), ())), preferred_element_type=jnp.float32
        )
        return raw.reshape(slots, inner)

    query_raw = project(w_query)
    key_raw = project(w_key)
    value_raw = project(w_value)
    query_hat, query_scale = head_norm(query_raw, HDIM)
    key_hat, key_scale = head_norm(key_raw, HDIM)
    query_b = query_hat.astype(jnp.bfloat16)
    key_b = key_hat.astype(jnp.bfloat16)
    value_b = value_raw.reshape(slots, heads_here, HDIM).astype(jnp.bfloat16)
    current = lax.broadcasted_iota(jnp.int32, (slots, slots), 0)
    earlier = lax.broadcasted_iota(jnp.int32, (slots, slots), 1)
    allowed = (earlier <= current) & ((all_present[None, :] > 0.5) | (earlier == current))
    scores = jnp.einsum("ihd,jhd->hij", query_b, key_b, preferred_element_type=jnp.float32) * scale
    exponent = jnp.where(allowed[None], jnp.exp(scores), 0.0)
    attend = exponent / jnp.sum(exponent, axis=-1, keepdims=True)
    attend_b = attend.astype(jnp.bfloat16)
    mixed = jnp.einsum("hij,jhd->ihd", attend_b, value_b, preferred_element_type=jnp.float32)
    mixed = mixed.astype(jnp.bfloat16).reshape(slots, inner)
    mixed_back = lax.dot_general(
        chunk_delta, w_out, (((2,), (1,)), ((), ())), preferred_element_type=jnp.float32
    )
    mixed_back = mixed_back.astype(jnp.bfloat16).reshape(slots, heads_here, HDIM)
    attend_back = jnp.einsum(
        "ihd,jhd->hij", mixed_back, value_b, preferred_element_type=jnp.float32
    )
    inner_sum = jnp.sum(attend * attend_back, axis=-1, keepdims=True)
    scores_back = (attend * (attend_back - inner_sum) * scale).astype(jnp.bfloat16)
    value_back = jnp.einsum(
        "hij,ihd->jhd", attend_b, mixed_back, preferred_element_type=jnp.float32
    )
    value_back = value_back.astype(jnp.bfloat16).reshape(slots, inner)
    qhat_back = jnp.einsum("hij,jhd->ihd", scores_back, key_b, preferred_element_type=jnp.float32)
    khat_back = jnp.einsum("hij,ihd->jhd", scores_back, query_b, preferred_element_type=jnp.float32)
    query_back = (
        norm_back(qhat_back, query_hat, query_scale).astype(jnp.bfloat16).reshape(slots, inner)
    )
    key_back = norm_back(khat_back, key_hat, key_scale).astype(jnp.bfloat16).reshape(slots, inner)
    mixed_late, query_back, key_back, value_back = lax.optimization_barrier(
        (mixed, query_back, key_back, value_back)
    )
    contributions = lax.dot_general(
        mixed_late.reshape(n_ctx, capacity, inner),
        w_out,
        (((2,), (0,)), ((), ())),
        preferred_element_type=jnp.float32,
    ).astype(jnp.bfloat16)
    received = lax.all_to_all(
        contributions, "ctx", 0, 0, tiled=True
    )
    update = jnp.sum(received.astype(jnp.float32), axis=0)
    scaled = weights[:, None] * update
    spread = jnp.sum(
        jnp.einsum("jt,kjd->ktd", onehot, bf16_pieces(scaled), preferred_element_type=jnp.float32),
        axis=0,
    )
    layer_out = (tokens[0].astype(jnp.float32) + spread).astype(jnp.bfloat16)[None]
    gate_back = jnp.sum(rows_back * update, axis=-1) * weights * (1.0 - weights)
    router_part = jnp.sum(
        jnp.dot(bf16_pieces(gate_back), rows.astype(jnp.bfloat16), preferred_element_type=jnp.float32),
        axis=0,
    )
    router_split = jnp.stack(
        [
            router_part.astype(jnp.bfloat16),
            (router_part - router_part.astype(jnp.bfloat16).astype(jnp.float32)).astype(
                jnp.bfloat16
            ),
        ]
    )
    router_group = jnp.sum(
        lax.all_gather(router_split, "ctx", axis=0, tiled=False).astype(jnp.float32), axis=(0, 1)
    )
    router_high = router_group.astype(jnp.bfloat16)
    router_low = (router_group - router_high.astype(jnp.float32)).astype(jnp.bfloat16)
    factors = lax.all_gather(
        jnp.concatenate([query_back, key_back, value_back], axis=1), "dp", axis=0, tiled=False
    ).reshape(n_dp * slots, 3 * inner)

    def contract(left, right):
        return lax.dot_general(
            left, right, (((0,), (0,)), ((), ())), preferred_element_type=jnp.float32
        ).astype(jnp.bfloat16)

    grads = contract(normed_blocks, factors)
    grad_query = grads[:, :inner]
    grad_key = grads[:, inner : 2 * inner]
    grad_value = grads[:, 2 * inner :]
    dp_index = lax.axis_index("dp")
    delta_by_seq = delta_blocks.reshape(n_dp, slots, block)
    out_total = lax.dot_general(
        mixed,
        lax.dynamic_index_in_dim(delta_by_seq, dp_index, 0, keepdims=False),
        (((0,), (0,)), ((), ())),
        preferred_element_type=jnp.float32,
    )
    for shift in range(1, n_dp):
        arrived = lax.ppermute(mixed, "dp", [(i, (i + shift) % n_dp) for i in range(n_dp)])
        source = (dp_index + n_dp - shift) % n_dp
        out_total = out_total + lax.dot_general(
            arrived,
            lax.dynamic_index_in_dim(delta_by_seq, source, 0, keepdims=False),
            (((0,), (0,)), ((), ())),
            preferred_element_type=jnp.float32,
        )
    grad_out = out_total.astype(jnp.bfloat16)
    router_pair = jnp.stack([router_high, router_low])
    router_pieces = lax.dynamic_update_index_in_dim(
        jnp.zeros((n_dp,) + router_pair.shape, jnp.bfloat16), router_pair, dp_index, 0
    )
    for shift in range(1, n_dp):
        arrived = lax.ppermute(router_pair, "dp", [(i, (i + shift) % n_dp) for i in range(n_dp)])
        router_pieces = lax.dynamic_update_index_in_dim(
            router_pieces, arrived, (dp_index + n_dp - shift) % n_dp, 0
        )
    router_pieces = router_pieces.astype(jnp.float32)
    grad_router = jnp.sum(router_pieces[:, 0] + router_pieces[:, 1], axis=0)
    return (layer_out, grad_query, grad_key, grad_value, grad_out, grad_router)


def solution(mesh):
    n_dp = mesh.shape["dp"]
    n_ctx = mesh.shape["ctx"]
    in_specs = (
        P("dp", "ctx", None),
        P("dp", "ctx", None),
        P(),
        P(None, "ctx"),
        P(None, "ctx"),
        P(None, "ctx"),
        P("ctx", None),
        P("dp", "ctx"),
        P("dp", "ctx"),
    )
    out_specs = (
        P("dp", "ctx", None),
        P("dp", "ctx"),
        P("dp", "ctx"),
        P("dp", "ctx"),
        P("ctx", "dp"),
        P(),
    )

    def run(*args):
        return body(n_dp, n_ctx, *args)

    return jax.shard_map(run, mesh=mesh, in_specs=in_specs, out_specs=out_specs, check_vma=False)
```

```python
import math

import jax
import jax.numpy as jnp
from jax import lax
from jax.sharding import PartitionSpec as P

HDIM = 128


HIGHEST_PRECISION = lax.Precision.HIGHEST


def head_norm(values, width):
    shaped = values.reshape(values.shape[0], -1, width)
    inverse = lax.rsqrt(jnp.mean(shaped * shaped, axis=-1, keepdims=True) + 1e-06)
    return (shaped * inverse, inverse)


def norm_back(grad_hat, normal, inverse):
    return inverse * (grad_hat - normal * jnp.mean(grad_hat * normal, axis=-1, keepdims=True))


def rounded_term(part):
    return lax.optimization_barrier(part.astype(jnp.bfloat16)).astype(jnp.float32)


def body(n_dp, n_ctx, tokens, cotangent, w_router, w_query, w_key, w_value, w_out, chosen, counts):
    length = tokens.shape[1]
    width = tokens.shape[2]
    capacity = chosen.shape[1]
    inner = w_query.shape[1]
    heads_here = inner // HDIM
    scale = 1.0 / math.sqrt(HDIM)
    offset = lax.axis_index("ctx") * length
    slot_ids = lax.broadcasted_iota(jnp.int32, (capacity,), 0)
    local = chosen[0] - offset
    present = (slot_ids < counts[0, 0]) & (local >= 0) & (local < length)
    columns = lax.broadcasted_iota(jnp.int32, (capacity, length), 1)
    onehot = ((local[:, None] == columns) & present[:, None]).astype(jnp.bfloat16)
    rows = jnp.dot(onehot, tokens[0], preferred_element_type=jnp.float32)
    rows_back = jnp.dot(onehot, cotangent[0], preferred_element_type=jnp.float32)
    logits = jnp.dot(rows, w_router, precision=HIGHEST_PRECISION)
    weights = jax.nn.sigmoid(logits)
    normed = (rows * lax.rsqrt(jnp.mean(rows * rows, axis=-1, keepdims=True) + 1e-05)).astype(
        jnp.bfloat16
    )
    delta = (weights[:, None] * rows_back).astype(jnp.bfloat16)
    flag_cols = jnp.zeros((capacity, HDIM), jnp.bfloat16).at[:, 0].set(
        present.astype(jnp.bfloat16)
    )
    packed = lax.all_gather(
        jnp.concatenate([normed, delta, flag_cols], axis=1), "ctx", axis=0, tiled=False
    )
    chunk_normed = packed[:, :, :width]
    chunk_delta = packed[:, :, width : 2 * width]
    all_present = packed[:, :, 2 * width].reshape(n_ctx * capacity)
    slots = n_ctx * capacity
    block = width // n_dp
    own_blocks = lax.all_to_all(
        jnp.concatenate([normed, delta], axis=0), "dp", 1, 0, tiled=True
    )
    pieces = lax.all_gather(own_blocks, "ctx", axis=0, tiled=False).reshape(
        n_ctx, n_dp, 2, capacity, block
    )
    normed_blocks = pieces[:, :, 0].transpose(1, 0, 2, 3).reshape(n_dp * slots, block)
    delta_blocks = pieces[:, :, 1].transpose(1, 0, 2, 3).reshape(n_dp * slots, block)
    def project(weight):
        raw = lax.dot_general(
            chunk_normed, weight, (((2,), (0,)), ((), ())), preferred_element_type=jnp.float32
        )
        return raw.reshape(slots, inner)

    query_raw = project(w_query)
    key_raw = project(w_key)
    value_raw = project(w_value)
    query_hat, query_scale = head_norm(query_raw, HDIM)
    key_hat, key_scale = head_norm(key_raw, HDIM)
    query_b = query_hat.astype(jnp.bfloat16)
    key_b = key_hat.astype(jnp.bfloat16)
    value_b = value_raw.reshape(slots, heads_here, HDIM).astype(jnp.bfloat16)
    current = lax.broadcasted_iota(jnp.int32, (slots, slots), 0)
    earlier = lax.broadcasted_iota(jnp.int32, (slots, slots), 1)
    allowed = (earlier <= current) & ((all_present[None, :] > 0.5) | (earlier == current))
    scores = jnp.einsum("ihd,jhd->hij", query_b, key_b, preferred_element_type=jnp.float32) * scale
    exponent = jnp.where(allowed[None], jnp.exp(scores), 0.0)
    attend = exponent / jnp.sum(exponent, axis=-1, keepdims=True)
    attend_b = attend.astype(jnp.bfloat16)
    mixed = jnp.einsum("hij,jhd->ihd", attend_b, value_b, preferred_element_type=jnp.float32)
    mixed = mixed.astype(jnp.bfloat16).reshape(slots, inner)
    mixed_back = lax.dot_general(
        chunk_delta, w_out, (((2,), (1,)), ((), ())), preferred_element_type=jnp.float32
    )
    mixed_back = mixed_back.astype(jnp.bfloat16).reshape(slots, heads_here, HDIM)
    attend_back = jnp.einsum(
        "ihd,jhd->hij", mixed_back, value_b, preferred_element_type=jnp.float32
    )
    inner_sum = jnp.sum(attend * attend_back, axis=-1, keepdims=True)
    scores_back = (attend * (attend_back - inner_sum) * scale).astype(jnp.bfloat16)
    value_back = jnp.einsum(
        "hij,ihd->jhd", attend_b, mixed_back, preferred_element_type=jnp.float32
    )
    value_back = value_back.astype(jnp.bfloat16).reshape(slots, inner)
    qhat_back = jnp.einsum("hij,jhd->ihd", scores_back, key_b, preferred_element_type=jnp.float32)
    khat_back = jnp.einsum("hij,ihd->jhd", scores_back, query_b, preferred_element_type=jnp.float32)
    query_back = (
        norm_back(qhat_back, query_hat, query_scale).astype(jnp.bfloat16).reshape(slots, inner)
    )
    key_back = norm_back(khat_back, key_hat, key_scale).astype(jnp.bfloat16).reshape(slots, inner)
    mixed_late, query_back, key_back, value_back = lax.optimization_barrier(
        (mixed, query_back, key_back, value_back)
    )
    contributions = lax.dot_general(
        mixed_late.reshape(n_ctx, capacity, inner),
        w_out,
        (((2,), (0,)), ((), ())),
        preferred_element_type=jnp.float32,
    ).astype(jnp.bfloat16)
    received = lax.all_to_all(
        contributions, "ctx", 0, 0, tiled=True
    )
    update = jnp.sum(received.astype(jnp.float32), axis=0)
    scaled = weights[:, None] * update
    spread = jnp.dot(onehot.astype(jnp.float32).T, scaled, precision=HIGHEST_PRECISION)
    layer_out = (tokens[0].astype(jnp.float32) + spread).astype(jnp.bfloat16)[None]
    gate_back = jnp.sum(rows_back * update, axis=-1) * weights * (1.0 - weights)
    router_part = jnp.dot(gate_back, rows, precision=HIGHEST_PRECISION)
    router_group = jnp.sum(lax.all_gather(router_part, "ctx", axis=0, tiled=False), axis=0)
    router_high = router_group.astype(jnp.bfloat16)
    router_low = (router_group - router_high.astype(jnp.float32)).astype(jnp.bfloat16)
    factors = lax.all_gather(
        jnp.concatenate([query_back, key_back, value_back], axis=1), "dp", axis=0, tiled=False
    ).reshape(n_dp * slots, 3 * inner)

    def contract(left, right):
        return lax.dot_general(
            left, right, (((0,), (0,)), ((), ())), preferred_element_type=jnp.float32
        ).astype(jnp.bfloat16)

    grads = contract(normed_blocks, factors)
    grad_query = grads[:, :inner]
    grad_key = grads[:, inner : 2 * inner]
    grad_value = grads[:, 2 * inner :]
    dp_index = lax.axis_index("dp")
    delta_by_seq = delta_blocks.reshape(n_dp, slots, block)
    out_total = lax.dot_general(
        mixed,
        lax.dynamic_index_in_dim(delta_by_seq, dp_index, 0, keepdims=False),
        (((0,), (0,)), ((), ())),
        preferred_element_type=jnp.float32,
    )
    for shift in range(1, n_dp):
        arrived = lax.ppermute(mixed, "dp", [(i, (i + shift) % n_dp) for i in range(n_dp)])
        source = (dp_index + n_dp - shift) % n_dp
        out_total = out_total + lax.dot_general(
            arrived,
            lax.dynamic_index_in_dim(delta_by_seq, source, 0, keepdims=False),
            (((0,), (0,)), ((), ())),
            preferred_element_type=jnp.float32,
        )
    grad_out = out_total.astype(jnp.bfloat16)
    router_pair = jnp.stack([router_high, router_low])
    router_pieces = lax.dynamic_update_index_in_dim(
        jnp.zeros((n_dp,) + router_pair.shape, jnp.bfloat16), router_pair, dp_index, 0
    )
    for shift in range(1, n_dp):
        arrived = lax.ppermute(router_pair, "dp", [(i, (i + shift) % n_dp) for i in range(n_dp)])
        router_pieces = lax.dynamic_update_index_in_dim(
            router_pieces, arrived, (dp_index + n_dp - shift) % n_dp, 0
        )
    router_pieces = router_pieces.astype(jnp.float32)
    grad_router = jnp.sum(router_pieces[:, 0] + router_pieces[:, 1], axis=0)
    return (layer_out, grad_query, grad_key, grad_value, grad_out, grad_router)


def solution(mesh):
    n_dp = mesh.shape["dp"]
    n_ctx = mesh.shape["ctx"]
    in_specs = (
        P("dp", "ctx", None),
        P("dp", "ctx", None),
        P(),
        P(None, "ctx"),
        P(None, "ctx"),
        P(None, "ctx"),
        P("ctx", None),
        P("dp", "ctx"),
        P("dp", "ctx"),
    )
    out_specs = (
        P("dp", "ctx", None),
        P("dp", "ctx"),
        P("dp", "ctx"),
        P("dp", "ctx"),
        P("ctx", "dp"),
        P(),
    )

    def run(*args):
        return body(n_dp, n_ctx, *args)

    return jax.shard_map(run, mesh=mesh, in_specs=in_specs, out_specs=out_specs, check_vma=False)
```

```python
import math

import jax
import jax.numpy as jnp
from jax import lax
from jax.sharding import PartitionSpec as P

HDIM = 128


HIGHEST_PRECISION = lax.Precision.HIGHEST


def head_norm(values, width):
    shaped = values.reshape(values.shape[0], -1, width)
    inverse = lax.rsqrt(jnp.mean(shaped * shaped, axis=-1, keepdims=True) + 1e-06)
    return (shaped * inverse, inverse)


def norm_back(grad_hat, normal, inverse):
    return inverse * (grad_hat - normal * jnp.mean(grad_hat * normal, axis=-1, keepdims=True))


def rounded_term(part):
    return lax.optimization_barrier(part.astype(jnp.bfloat16)).astype(jnp.float32)


def body(n_dp, n_ctx, tokens, cotangent, w_router, w_query, w_key, w_value, w_out, chosen, counts):
    length = tokens.shape[1]
    width = tokens.shape[2]
    capacity = chosen.shape[1]
    inner = w_query.shape[1]
    heads_here = inner // HDIM
    scale = 1.0 / math.sqrt(HDIM)
    offset = lax.axis_index("ctx") * length
    slot_ids = lax.broadcasted_iota(jnp.int32, (capacity,), 0)
    local = chosen[0] - offset
    present = (slot_ids < counts[0, 0]) & (local >= 0) & (local < length)
    columns = lax.broadcasted_iota(jnp.int32, (capacity, length), 1)
    onehot = ((local[:, None] == columns) & present[:, None]).astype(jnp.bfloat16)
    rows = jnp.dot(onehot, tokens[0], preferred_element_type=jnp.float32)
    rows_back = jnp.dot(onehot, cotangent[0], preferred_element_type=jnp.float32)
    logits = jnp.dot(rows, w_router, precision=HIGHEST_PRECISION)
    weights = jax.nn.sigmoid(logits)
    normed = (rows * lax.rsqrt(jnp.mean(rows * rows, axis=-1, keepdims=True) + 1e-05)).astype(
        jnp.bfloat16
    )
    delta = (weights[:, None] * rows_back).astype(jnp.bfloat16)
    flag_cols = jnp.zeros((capacity, HDIM), jnp.bfloat16).at[:, 0].set(
        present.astype(jnp.bfloat16)
    )
    packed = lax.all_gather(
        jnp.concatenate([normed, delta, flag_cols], axis=1), "ctx", axis=0, tiled=False
    )
    chunk_normed = packed[:, :, :width]
    chunk_delta = packed[:, :, width : 2 * width]
    all_present = packed[:, :, 2 * width].reshape(n_ctx * capacity)
    slots = n_ctx * capacity
    block = width // n_dp
    own_blocks = lax.all_to_all(
        jnp.concatenate([normed, delta], axis=0), "dp", 1, 0, tiled=True
    )
    pieces = lax.all_gather(own_blocks, "ctx", axis=0, tiled=False).reshape(
        n_ctx, n_dp, 2, capacity, block
    )
    normed_blocks = pieces[:, :, 0].transpose(1, 0, 2, 3).reshape(n_dp * slots, block)
    delta_blocks = pieces[:, :, 1].transpose(1, 0, 2, 3).reshape(n_dp * slots, block)
    def project(weight):
        raw = lax.dot_general(
            chunk_normed, weight, (((2,), (0,)), ((), ())), preferred_element_type=jnp.float32
        )
        return raw.reshape(slots, inner)

    query_raw = project(w_query)
    key_raw = project(w_key)
    value_raw = project(w_value)
    query_hat, query_scale = head_norm(query_raw, HDIM)
    key_hat, key_scale = head_norm(key_raw, HDIM)
    query_b = query_hat.astype(jnp.bfloat16)
    key_b = key_hat.astype(jnp.bfloat16)
    value_b = value_raw.reshape(slots, heads_here, HDIM).astype(jnp.bfloat16)
    current = lax.broadcasted_iota(jnp.int32, (slots, slots), 0)
    earlier = lax.broadcasted_iota(jnp.int32, (slots, slots), 1)
    allowed = (earlier <= current) & ((all_present[None, :] > 0.5) | (earlier == current))
    scores = jnp.einsum("ihd,jhd->hij", query_b, key_b, preferred_element_type=jnp.float32) * scale
    exponent = jnp.where(allowed[None], jnp.exp(scores), 0.0)
    attend = exponent / jnp.sum(exponent, axis=-1, keepdims=True)
    attend_b = attend.astype(jnp.bfloat16)
    mixed = jnp.einsum("hij,jhd->ihd", attend_b, value_b, preferred_element_type=jnp.float32)
    mixed = mixed.astype(jnp.bfloat16).reshape(slots, inner)
    mixed_back = lax.dot_general(
        chunk_delta, w_out, (((2,), (1,)), ((), ())), preferred_element_type=jnp.float32
    )
    mixed_back = mixed_back.astype(jnp.bfloat16).reshape(slots, heads_here, HDIM)
    attend_back = jnp.einsum(
        "ihd,jhd->hij", mixed_back, value_b, preferred_element_type=jnp.float32
    )
    inner_sum = jnp.sum(attend * attend_back, axis=-1, keepdims=True)
    scores_back = (attend * (attend_back - inner_sum) * scale).astype(jnp.bfloat16)
    value_back = jnp.einsum(
        "hij,ihd->jhd", attend_b, mixed_back, preferred_element_type=jnp.float32
    )
    value_back = value_back.astype(jnp.bfloat16).reshape(slots, inner)
    qhat_back = jnp.einsum("hij,jhd->ihd", scores_back, key_b, preferred_element_type=jnp.float32)
    khat_back = jnp.einsum("hij,ihd->jhd", scores_back, query_b, preferred_element_type=jnp.float32)
    query_back = (
        norm_back(qhat_back, query_hat, query_scale).astype(jnp.bfloat16).reshape(slots, inner)
    )
    key_back = norm_back(khat_back, key_hat, key_scale).astype(jnp.bfloat16).reshape(slots, inner)
    mixed_late, query_back, key_back, value_back = lax.optimization_barrier(
        (mixed, query_back, key_back, value_back)
    )
    contributions = lax.dot_general(
        mixed_late.reshape(n_ctx, capacity, inner),
        w_out,
        (((2,), (0,)), ((), ())),
        preferred_element_type=jnp.float32,
    ).astype(jnp.bfloat16)
    received = lax.all_to_all(
        contributions, "ctx", 0, 0, tiled=True
    )
    update = jnp.sum(received.astype(jnp.float32), axis=0)
    scaled = weights[:, None] * update
    spread = jnp.dot(onehot.astype(jnp.float32).T, scaled, precision=HIGHEST_PRECISION)
    layer_out = (tokens[0].astype(jnp.float32) + spread).astype(jnp.bfloat16)[None]
    gate_back = jnp.sum(rows_back * update, axis=-1) * weights * (1.0 - weights)
    router_part = jnp.dot(gate_back, rows, precision=HIGHEST_PRECISION)
    router_group = jnp.sum(lax.all_gather(router_part, "ctx", axis=0, tiled=False), axis=0)
    factors = lax.all_gather(
        jnp.concatenate([query_back, key_back, value_back], axis=1), "dp", axis=0, tiled=False
    ).reshape(n_dp * slots, 3 * inner)

    def contract(left, right):
        return lax.dot_general(
            left, right, (((0,), (0,)), ((), ())), preferred_element_type=jnp.float32
        ).astype(jnp.bfloat16)

    grads = contract(normed_blocks, factors)
    grad_query = grads[:, :inner]
    grad_key = grads[:, inner : 2 * inner]
    grad_value = grads[:, 2 * inner :]
    dp_index = lax.axis_index("dp")
    delta_by_seq = delta_blocks.reshape(n_dp, slots, block)
    out_total = lax.dot_general(
        mixed,
        lax.dynamic_index_in_dim(delta_by_seq, dp_index, 0, keepdims=False),
        (((0,), (0,)), ((), ())),
        preferred_element_type=jnp.float32,
    )
    for shift in range(1, n_dp):
        arrived = lax.ppermute(mixed, "dp", [(i, (i + shift) % n_dp) for i in range(n_dp)])
        source = (dp_index + n_dp - shift) % n_dp
        out_total = out_total + lax.dot_general(
            arrived,
            lax.dynamic_index_in_dim(delta_by_seq, source, 0, keepdims=False),
            (((0,), (0,)), ((), ())),
            preferred_element_type=jnp.float32,
        )
    grad_out = out_total.astype(jnp.bfloat16)
    router_pieces = lax.dynamic_update_index_in_dim(
        jnp.zeros((n_dp,) + router_group.shape, jnp.float32), router_group, dp_index, 0
    )
    for shift in range(1, n_dp):
        arrived = lax.ppermute(router_group, "dp", [(i, (i + shift) % n_dp) for i in range(n_dp)])
        router_pieces = lax.dynamic_update_index_in_dim(
            router_pieces, arrived, (dp_index + n_dp - shift) % n_dp, 0
        )
    grad_router = jnp.sum(router_pieces, axis=0)
    return (layer_out, grad_query, grad_key, grad_value, grad_out, grad_router)


def solution(mesh):
    n_dp = mesh.shape["dp"]
    n_ctx = mesh.shape["ctx"]
    in_specs = (
        P("dp", "ctx", None),
        P("dp", "ctx", None),
        P(),
        P(None, "ctx"),
        P(None, "ctx"),
        P(None, "ctx"),
        P("ctx", None),
        P("dp", "ctx"),
        P("dp", "ctx"),
    )
    out_specs = (
        P("dp", "ctx", None),
        P("dp", "ctx"),
        P("dp", "ctx"),
        P("dp", "ctx"),
        P("ctx", "dp"),
        P(),
    )

    def run(*args):
        return body(n_dp, n_ctx, *args)

    return jax.shard_map(run, mesh=mesh, in_specs=in_specs, out_specs=out_specs, check_vma=False)
```
